128 devices in a mesh: ctl: 32 (over y, z_lo, x), side: 2 (over core), tp: 2 (over z_hi).
Axes of the slice: x: 4, y: 4, z: 4 (z_hi: 2, z_lo: 2; z = z_hi * 2 + z_lo), core: 2. Of those that a mesh axis runs over, the one named last changes fastest.
Arguments:
- image_latent: bfloat16 [64, 256, 3072], P('ctl'), may hold values from -6 to 6
- control_latent: bfloat16 [64, 256, 3072], P('ctl'), may hold values from -6 to 6
- control_order: int32 [64, 256], P('ctl'), may hold values from 0 to 255, each once within a row
- captions: bfloat16 [128, 128, 3072], P('ctl'), may hold values from -6 to 6
- caption_ids: int32 [64], P('ctl'), may hold values from 0 to 3
- modulation: float32 [2, 64, 3, 3072], P('side', 'ctl'), may hold values from -3 to 3
- qkv_weight: bfloat16 [2, 3072, 3, 1536], P('side', 'ctl', None, 'tp'), may hold values from -1 to 1
- qk_gain: float32 [2, 2, 128], P('side'), may hold values from 1 to 6
- out_weight: bfloat16 [2, 1536, 3072], P('side', 'tp', 'ctl'), may hold values from -0.5 to 0.5
- zero_weight: bfloat16 [3072, 3072], P('ctl', 'tp'), may hold values from -0.109375 to 0.109375
- proj_weight: bfloat16 [3072, 64], P('tp'), may hold values from -1 to 1
- final_mod: float32 [64, 2, 3072], P('ctl'), may hold values from -3 to 3
- velocity_target: float32 [64, 256, 64], P('ctl'), may hold values from -6 to 6
Outputs:
- hidden_out: bfloat16 [2, 64, 256, 3072], P('side', 'ctl', None, 'tp')
- zero_grad: float32 [3072, 3072], P(('ctl', 'side'), 'tp')
The draws below stay inside these ranges and needn't reach their ends.
Inputs may be any that keep to these rules, and one draw needn't show every extreme that they name: caption_ids counts from the first caption held by the sample's own index of ctl. Each sample's row of control_order is a permutation.
All inputs are finite; a program needn't handle non-finite values.
Results may differ from the reference program's by a relative error of at most 0.03.
Values may be sent and summed in bfloat16 or wider, within the bound.
No kernel may reach another device: no remote copies, remote signals or barrier semaphores. Data moves between devices by JAX's collectives and lax.ppermute only.
A program may use at most 192 MiB of HBM per device.

```python
import math
import jax
import jax.numpy as jnp
from jax import lax

D = 3072
HEADS = 12
HEAD_DIM = 128
OUT_CH = 64
HDIM = 1536
IMG = 256
TXT = 128
MB = 2
CAP_DEV = 4
SAMPLES = 64
CAPTIONS = 128
N_CTL = 32
N_TP = 2


def feature_ramp(low_end, high_end):
    place = jnp.arange(D, dtype=jnp.float32) / float(D - 1)
    return jnp.exp(math.log(low_end) + (math.log(high_end) - math.log(low_end)) * place)


def draw_image_latent(key, part):
    own_key = jax.random.fold_in(key, 101)
    drawn = jax.random.normal(own_key, (SAMPLES, IMG, D), jnp.float32)
    drawn = drawn * feature_ramp(0.4, 2.5)
    return jnp.clip(drawn, -6.0, 6.0).astype(jnp.bfloat16)


def draw_control_latent(key, part):
    own_key = jax.random.fold_in(key, 202)
    drawn = jax.random.normal(own_key, (SAMPLES, IMG, D), jnp.float32)
    return jnp.clip(drawn, -6.0, 6.0).astype(jnp.bfloat16)


def draw_qkv_weight(key, part):
    own_key = jax.random.fold_in(key, 303)
    drawn = jax.random.normal(own_key, (2, D, 3, HEADS, HEAD_DIM), jnp.float32) / math.sqrt(D)
    return jnp.clip(drawn, -1.0, 1.0).reshape(2, D, 3, HEADS * HEAD_DIM).astype(jnp.bfloat16)


def draw_qk_gain(key, part):
    own_key = jax.random.fold_in(key, 404)
    return jax.random.uniform(own_key, (2, 2, HEAD_DIM), jnp.float32, 1.0, 2.0)


def draw_proj_weight(key, part):
    own_key = jax.random.fold_in(key, 505)
    drawn = jax.random.normal(own_key, (D, OUT_CH), jnp.float32) / math.sqrt(D)
    drawn = drawn * feature_ramp(0.5, 2.0)[:, None]
    return jnp.clip(drawn, -1.0, 1.0).astype(jnp.bfloat16)


def touch_ends(array, key, least, largest):
    shape = array.shape
    index_at = [jax.random.randint(jax.random.fold_in(key, axis), (), 0, shape[axis]) for axis in range(len(shape))]
    array = array.at[tuple(index_at)].set(least)
    longest = shape.index(max(shape))
    index_at[longest] = (index_at[longest] + 1) % shape[longest]
    return array.at[tuple(index_at)].set(largest)


def block_levels(key, dims, cuts, low, high):
    factor_of, own = 1.0, jax.random.fold_in(key, 6)
    for axis_at, blocks in cuts:
        steps = jnp.exp(jax.random.uniform(jax.random.fold_in(own, axis_at), (blocks,), jnp.float32, low / len(cuts), high / len(cuts)))
        factor_of = factor_of * jnp.repeat(steps, dims[axis_at] // blocks).reshape([-1 if axis == axis_at else 1 for axis in range(len(dims))])
    return factor_of


def centred(rng, dims, width, reach, split=(), kind=jnp.bfloat16):
    level = block_levels(rng, dims, split, -0.22, 0.18) if split else 1.0
    entries = jax.random.normal(rng, dims, jnp.float32) * width * level
    return jnp.minimum(jnp.maximum(entries, -reach), reach).astype(kind)


def setup_inputs(seed: int = 0) -> dict:
    splits = jax.random.split(jax.random.key(seed), 14)
    image_latent = draw_image_latent(jax.random.fold_in(splits[13], 71), 0)
    control_latent = draw_control_latent(jax.random.fold_in(splits[13], 71), 0)
    control_order = jax.vmap(lambda own: jax.random.permutation(own, IMG))(jax.random.split(splits[2], SAMPLES)).reshape((SAMPLES, IMG)).astype(jnp.int32)
    captions = centred(splits[3], (CAPTIONS, TXT, D), 1.0, 6.0, ((0, 32),))
    caption_ids = touch_ends(jax.random.randint(splits[4], (SAMPLES,), 0, CAP_DEV), jax.random.fold_in(splits[4], 1), 0, CAP_DEV - 1).astype(jnp.int32)
    modulation = centred(splits[5], (2, SAMPLES, 3, D), 0.7, 3.0, ((0, 2), (1, 32)), jnp.float32)
    qkv_weight = draw_qkv_weight(jax.random.fold_in(splits[13], 71), 0)
    qk_gain = draw_qk_gain(jax.random.fold_in(splits[13], 71), 0)
    out_weight = centred(splits[8], (2, HDIM, D), HEAD_DIM ** -0.5, 0.5, ((0, 2), (1, 2), (2, 32)))
    zero_weight = centred(splits[9], (D, D), D ** -0.5, 0.109375, ((0, 32), (1, 2)))
    proj_weight = draw_proj_weight(jax.random.fold_in(splits[13], 71), 0)
    final_mod = centred(splits[11], (SAMPLES, 2, D), 0.5, 3.0, ((0, 32),), jnp.float32)
    velocity_target = centred(splits[12], (SAMPLES, IMG, OUT_CH), 1.0, 6.0, ((0, 32),), jnp.float32)
    return dict(image_latent=image_latent, control_latent=control_latent, control_order=control_order, captions=captions, caption_ids=caption_ids, modulation=modulation, qkv_weight=qkv_weight, qk_gain=qk_gain, out_weight=out_weight, zero_weight=zero_weight, proj_weight=proj_weight, final_mod=final_mod, velocity_target=velocity_target)


EPS = 1e-06

def layer_norm(values):
    center = values - lax.optimization_barrier(jnp.mean(values, axis=-1, keepdims=True))
    spread = lax.optimization_barrier(jnp.mean(center * center, axis=-1, keepdims=True))
    return center * lax.rsqrt(spread + EPS)

def head_norm(values, gain_row):
    power_mean = lax.optimization_barrier(jnp.mean(values * values, axis=-1, keepdims=True))
    return (values * lax.rsqrt(power_mean + EPS) * gain_row).astype(jnp.bfloat16)

def section_pass(hidden, caption, modulate, weight, gain_pair, out_proj):
    sequence = jnp.concatenate([caption.astype(jnp.float32), hidden], axis=0)
    normed = (layer_norm(sequence) * (1.0 + modulate[1]) + modulate[0]).astype(jnp.bfloat16)
    queries = jnp.dot(normed[TXT:], weight[:, 0], preferred_element_type=jnp.float32)
    keys_all = jnp.dot(normed, weight[:, 1], preferred_element_type=jnp.float32)
    values_all = jnp.dot(normed, weight[:, 2], preferred_element_type=jnp.float32)
    queries = head_norm(queries.reshape(IMG, HEADS, HEAD_DIM), gain_pair[0])
    keys_all = head_norm(keys_all.reshape(TXT + IMG, HEADS, HEAD_DIM), gain_pair[1])
    values_all = values_all.astype(jnp.bfloat16).reshape(TXT + IMG, HEADS, HEAD_DIM)
    scores = jnp.einsum('ihd,jhd->hij', queries.astype(jnp.float32), keys_all.astype(jnp.float32)) / math.sqrt(HEAD_DIM)
    attend = jax.nn.softmax(scores, axis=-1).astype(jnp.bfloat16)
    mixed_heads = jnp.einsum('hij,jhd->ihd', attend.astype(jnp.float32), values_all.astype(jnp.float32))
    mixed_heads = mixed_heads.astype(jnp.bfloat16).reshape(IMG, HEADS * HEAD_DIM)
    width_part = HEADS * HEAD_DIM // N_TP
    attention = jnp.zeros((IMG, D), jnp.float32)
    for tp_slot in range(N_TP):
        low = tp_slot * width_part
        partial_value = jnp.dot(mixed_heads[:, low:low + width_part], out_proj[low:low + width_part], preferred_element_type=jnp.float32)
        narrow = lax.optimization_barrier(partial_value.astype(jnp.bfloat16))
        attention = attention + narrow.astype(jnp.float32)
    return hidden + modulate[2] * attention

def reference(image_latent, control_latent, control_order, captions, caption_ids, modulation, qkv_weight, qk_gain, out_weight, zero_weight, proj_weight, final_mod, velocity_target):
    loss_factor = 4.0 / math.sqrt(SAMPLES * IMG)

    def one_sample(sample):
        group_index = sample // MB
        caption = captions[group_index * CAP_DEV + caption_ids[sample]]
        aligned = jnp.take(control_latent[sample], control_order[sample], axis=0).astype(jnp.float32)
        plain_rows = image_latent[sample].astype(jnp.float32)
        control_act = section_pass(plain_rows + aligned, caption, modulation[0, sample], qkv_weight[0], qk_gain[0], out_weight[0])
        base_act = section_pass(plain_rows, caption, modulation[1, sample], qkv_weight[1], qk_gain[1], out_weight[1])
        act_narrow = control_act.astype(jnp.bfloat16)
        residual = jnp.dot(act_narrow, zero_weight, preferred_element_type=jnp.float32).astype(jnp.bfloat16)
        merged = base_act + residual.astype(jnp.float32)
        row_total = lax.optimization_barrier(jnp.sum(merged, axis=-1, keepdims=True))
        squares = lax.optimization_barrier(jnp.sum(merged * merged, axis=-1, keepdims=True))
        mean_val = row_total / D
        spread = squares / D - mean_val * mean_val
        scale_inv = lax.rsqrt(spread + EPS)
        unit_rows = (merged - mean_val) * scale_inv
        final_in = (unit_rows * (1.0 + final_mod[sample, 1]) + final_mod[sample, 0]).astype(jnp.bfloat16)
        prediction = jnp.dot(final_in, proj_weight, preferred_element_type=jnp.float32)
        grad_pred = (loss_factor * (prediction - velocity_target[sample])).astype(jnp.bfloat16)
        grad_unit = jnp.dot(grad_pred, proj_weight.T, preferred_element_type=jnp.float32) * (1.0 + final_mod[sample, 1])
        first_mean = lax.optimization_barrier(jnp.sum(grad_unit, axis=-1, keepdims=True)) / D
        second = lax.optimization_barrier(jnp.sum(grad_unit * unit_rows, axis=-1, keepdims=True)) / D
        grad_narrow = ((grad_unit - first_mean - unit_rows * second) * scale_inv).astype(jnp.bfloat16)
        return (residual, merged.astype(jnp.bfloat16), act_narrow, grad_narrow)
    residuals, merged_all, act_list, grad_list = lax.map(one_sample, jnp.arange(SAMPLES, dtype=jnp.int32))

    def group_term(running, group_index):
        rows_narrow = lax.dynamic_slice_in_dim(act_list, group_index * MB, MB, 0).reshape(MB * IMG, D)
        grads_narrow = lax.dynamic_slice_in_dim(grad_list, group_index * MB, MB, 0).reshape(MB * IMG, D)
        group_part = jnp.dot(rows_narrow.T, grads_narrow, preferred_element_type=jnp.float32)
        narrow = lax.optimization_barrier(group_part.astype(jnp.bfloat16))
        return (running + narrow.astype(jnp.float32), None)
    zero_grad, _ = lax.scan(group_term, jnp.zeros((D, D), jnp.float32), jnp.arange(N_CTL, dtype=jnp.int32))
    hidden_out = jnp.stack([residuals, merged_all], axis=0)
    return (hidden_out, zero_grad)
```

```python
import math

import jax
import jax.numpy as jnp
from jax import lax
from jax.sharding import PartitionSpec as P

HEAD_DIM = 128


EPS = 1e-06


def passed_along(shard, axis, by):
    length = lax.axis_size(axis)
    pairs = [(i, i + by) for i in range(length) if 0 <= i + by < length]
    return lax.ppermute(shard, axis, pairs)


def partner(value, axis, bit):
    mask = 2**bit
    pairs = [(source, source ^ mask) for source in range(lax.axis_size(axis))]
    return lax.ppermute(value, axis, pairs)


def swap(value, axis):
    return lax.ppermute(value, axis, [(0, 1), (1, 0)])


def layer_norm(values):
    center = values - jnp.mean(values, axis=-1, keepdims=True)
    spread = jnp.mean(center * center, axis=-1, keepdims=True)
    return center * lax.rsqrt(spread + EPS)


def head_norm(values, gain_row):
    power_mean = jnp.mean(values * values, axis=-1, keepdims=True)
    return (values * lax.rsqrt(power_mean + EPS) * gain_row).astype(jnp.bfloat16)


def rounded(values):
    narrow = lax.optimization_barrier(values.astype(jnp.bfloat16))
    return narrow.astype(jnp.float32)


def local(
    image_latent,
    control_latent,
    control_order,
    captions,
    caption_ids,
    modulation,
    qkv_weight,
    qk_gain,
    out_weight,
    zero_weight,
    proj_weight,
    final_mod,
    velocity_target,
):
    side_index = lax.axis_index("side")
    tp_index = lax.axis_index("tp")
    ctl_count = lax.axis_size("ctl")
    tp_count = lax.axis_size("tp")
    is_control = side_index == 0
    micro_count, img_rows, width_full = image_latent.shape
    text_rows = captions.shape[1]
    seq_rows = text_rows + img_rows
    local_heads = qkv_weight.shape[3]
    head_count = local_heads // HEAD_DIM
    half_width = width_full // tp_count
    quarter_width = half_width // 2
    flat_rows = micro_count * img_rows
    block_rows = width_full // (2 * ctl_count)
    aligned = jax.vmap(lambda latent, order_row: jnp.take(latent, order_row, axis=0))(
        control_latent, control_order
    )
    plain_rows = image_latent.astype(jnp.float32)
    hidden = plain_rows + jnp.where(is_control, 1.0, 0.0) * aligned.astype(jnp.float32)
    chosen = jnp.take(captions, caption_ids, axis=0).astype(jnp.float32)
    sequence = jnp.concatenate([chosen, hidden], axis=1)
    modulate = modulation[0]
    normed = (layer_norm(sequence) * (1.0 + modulate[:, 1:2]) + modulate[:, 0:1]).astype(
        jnp.bfloat16
    )
    text_flat = normed.reshape(micro_count * seq_rows, width_full)
    image_flat = normed[:, text_rows:].reshape(flat_rows, width_full)
    local_rows = qkv_weight.shape[1]
    own_cols = lax.dynamic_slice_in_dim(zero_weight, side_index * quarter_width, quarter_width, 1)
    packed = jnp.concatenate(
        [
            qkv_weight[0].reshape(local_rows, 3 * local_heads),
            out_weight[0].T,
            own_cols,
        ],
        axis=1,
    )
    gathered = lax.all_gather(packed, "ctl", axis=0, tiled=True)
    count_rows = gathered.shape[0]
    query_weight = gathered[:, :local_heads]
    pair_weight = gathered[:, local_heads : 3 * local_heads]
    out_cols = gathered[:, 3 * local_heads : 4 * local_heads]
    zero_cols = gathered[:, 4 * local_heads :]
    query_acc = jnp.dot(image_flat, query_weight, preferred_element_type=jnp.float32)
    pair_acc = jnp.dot(text_flat, pair_weight, preferred_element_type=jnp.float32)
    gain_pair = qk_gain[0]
    queries = head_norm(
        query_acc.reshape(micro_count, img_rows, head_count, HEAD_DIM), gain_pair[0]
    )
    pair_acc = pair_acc.reshape(micro_count, seq_rows, 2, head_count, HEAD_DIM)
    keys_all = head_norm(pair_acc[:, :, 0], gain_pair[1])
    values_all = pair_acc[:, :, 1].astype(jnp.bfloat16)
    scores = jnp.einsum(
        "bihd,bjhd->bhij", queries, keys_all, preferred_element_type=jnp.float32
    ) / math.sqrt(HEAD_DIM)
    attend = jax.nn.softmax(scores, axis=-1).astype(jnp.bfloat16)
    mixed_heads = jnp.einsum(
        "bhij,bjhd->bihd", attend, values_all, preferred_element_type=jnp.float32
    )
    mixed_heads = mixed_heads.astype(jnp.bfloat16).reshape(flat_rows, local_heads)
    contract_last = (((1,), (1,)), ((), ()))
    other_out = lax.dynamic_slice_in_dim(out_cols, (1 - tp_index) * half_width, half_width, 0)
    own_out = lax.dynamic_slice_in_dim(out_cols, tp_index * half_width, half_width, 0)
    other_part = lax.dot_general(
        mixed_heads, other_out, contract_last, preferred_element_type=jnp.float32
    ).astype(jnp.bfloat16)
    got_part = swap(other_part, "tp")
    own_part_heads = rounded(
        lax.dot_general(mixed_heads, own_out, contract_last, preferred_element_type=jnp.float32)
    )
    head_sum = own_part_heads + got_part.astype(jnp.float32)
    hid_half = lax.dynamic_slice_in_dim(hidden, tp_index * half_width, half_width, 2)
    gate_half = lax.dynamic_slice_in_dim(modulate[:, 2:3], tp_index * half_width, half_width, 2)
    act_half = hid_half + gate_half * head_sum.reshape(micro_count, img_rows, half_width)
    act_half = act_half.reshape(flat_rows, half_width)
    act_own = act_half.astype(jnp.bfloat16)
    act_got = swap(act_own, "tp")
    act_narrow = jnp.where(
        tp_index == 0,
        jnp.concatenate([act_own, act_got], axis=1),
        jnp.concatenate([act_got, act_own], axis=1),
    )
    act_other = passed_along(act_narrow, "side", 1)
    control_rows = jnp.where(is_control, act_narrow, act_other)
    own_part = jnp.dot(control_rows, zero_cols, preferred_element_type=jnp.float32)
    own_narrow = own_part.astype(jnp.bfloat16)
    other_narrow = partner(own_narrow, "side", 0)
    residual_narrow = jnp.where(
        is_control,
        jnp.concatenate([own_narrow, other_narrow], axis=1),
        jnp.concatenate([other_narrow, own_narrow], axis=1),
    )
    merged = act_half + residual_narrow.astype(jnp.float32)
    section_out = jnp.where(is_control, residual_narrow, merged.astype(jnp.bfloat16))
    final_half = lax.dynamic_slice_in_dim(final_mod, tp_index * half_width, half_width, 2)
    merged_rows = merged.reshape(micro_count, img_rows, half_width)
    row_total, squares = lax.psum(
        (
            jnp.sum(merged_rows, axis=-1, keepdims=True),
            jnp.sum(merged_rows * merged_rows, axis=-1, keepdims=True),
        ),
        "tp",
    )
    mean_val = row_total / width_full
    spread = squares / width_full - mean_val * mean_val
    scale_inv = lax.rsqrt(spread + EPS)
    unit_rows = (merged_rows - mean_val) * scale_inv
    final_in = (unit_rows * (1.0 + final_half[:, 1:2]) + final_half[:, 0:1]).astype(jnp.bfloat16)
    pred_part = jnp.dot(
        final_in.reshape(flat_rows, half_width), proj_weight, preferred_element_type=jnp.float32
    )
    prediction = pred_part + swap(pred_part, "tp")
    loss_factor = 4.0 / math.sqrt(micro_count * ctl_count * img_rows)
    grad_pred = (loss_factor * (prediction - velocity_target.reshape(flat_rows, -1))).astype(
        jnp.bfloat16
    )
    grad_unit = lax.dot_general(
        grad_pred, proj_weight, (((1,), (1,)), ((), ())), preferred_element_type=jnp.float32
    )
    grad_unit = grad_unit.reshape(micro_count, img_rows, half_width) * (1.0 + final_half[:, 1:2])
    first_sum, second_sum = lax.psum(
        (
            jnp.sum(grad_unit, axis=-1, keepdims=True),
            jnp.sum(grad_unit * unit_rows, axis=-1, keepdims=True),
        ),
        "tp",
    )
    grad_narrow = (
        (grad_unit - first_sum / width_full - unit_rows * (second_sum / width_full)) * scale_inv
    ).astype(jnp.bfloat16)
    grad_narrow = grad_narrow.reshape(flat_rows, half_width)
    returned = passed_along(grad_narrow, "side", -1)
    grad_rows_all = jnp.where(is_control, returned, grad_narrow)
    own_act = lax.dynamic_index_in_dim(
        control_rows.reshape(flat_rows, ctl_count, 2, block_rows), side_index, 2, keepdims=False
    )
    own_act = own_act.reshape(flat_rows, ctl_count * block_rows)
    product = lax.dot_general(
        own_act, grad_rows_all, (((0,), (0,)), ((), ())), preferred_element_type=jnp.float32
    )
    group_parts = rounded(product).astype(jnp.bfloat16).reshape(ctl_count, block_rows, half_width)
    received = lax.all_to_all(group_parts, "ctl", 0, 0, tiled=True)
    zero_grad = jnp.sum(received.astype(jnp.float32), axis=0)
    return (section_out.reshape(1, micro_count, img_rows, half_width), zero_grad)


def solution(mesh):
    return jax.shard_map(
        local,
        mesh=mesh,
        in_specs=(
            P("ctl", None, None),
            P("ctl", None, None),
            P("ctl", None),
            P("ctl", None, None),
            P("ctl"),
            P("side", "ctl", None, None),
            P("side", "ctl", None, "tp"),
            P("side", None, None),
            P("side", "tp", "ctl"),
            P("ctl", "tp"),
            P("tp", None),
            P("ctl", None, None),
            P("ctl", None, None),
        ),
        out_specs=(P("side", "ctl", None, "tp"), P(("ctl", "side"), "tp")),
        check_vma=False,
    )
```

```python
import math

import jax
import jax.numpy as jnp
from jax import lax
from jax.sharding import PartitionSpec as P

HEAD_DIM = 128


EPS = 1e-06


def passed_along(shard, axis, by):
    length = lax.axis_size(axis)
    pairs = [(i, i + by) for i in range(length) if 0 <= i + by < length]
    return lax.ppermute(shard, axis, pairs)


def partner(value, axis, bit):
    mask = 2**bit
    pairs = [(source, source ^ mask) for source in range(lax.axis_size(axis))]
    return lax.ppermute(value, axis, pairs)


def swap(value, axis):
    return lax.ppermute(value, axis, [(0, 1), (1, 0)])


def layer_norm(values):
    center = values - jnp.mean(values, axis=-1, keepdims=True)
    spread = jnp.mean(center * center, axis=-1, keepdims=True)
    return center * lax.rsqrt(spread + EPS)


def head_norm(values, gain_row):
    power_mean = jnp.mean(values * values, axis=-1, keepdims=True)
    return (values * lax.rsqrt(power_mean + EPS) * gain_row).astype(jnp.bfloat16)


def rounded(values):
    narrow = lax.optimization_barrier(values.astype(jnp.bfloat16))
    return narrow.astype(jnp.float32)


def local(
    image_latent,
    control_latent,
    control_order,
    captions,
    caption_ids,
    modulation,
    qkv_weight,
    qk_gain,
    out_weight,
    zero_weight,
    proj_weight,
    final_mod,
    velocity_target,
):
    side_index = lax.axis_index("side")
    tp_index = lax.axis_index("tp")
    ctl_count = lax.axis_size("ctl")
    tp_count = lax.axis_size("tp")
    is_control = side_index == 0
    micro_count, img_rows, width_full = image_latent.shape
    text_rows = captions.shape[1]
    seq_rows = text_rows + img_rows
    local_heads = qkv_weight.shape[3]
    head_count = local_heads // HEAD_DIM
    half_width = width_full // tp_count
    quarter_width = half_width // 2
    flat_rows = micro_count * img_rows
    block_rows = width_full // (2 * ctl_count)
    aligned = jax.vmap(lambda latent, order_row: jnp.take(latent, order_row, axis=0))(
        control_latent, control_order
    )
    plain_rows = image_latent.astype(jnp.float32)
    hidden = plain_rows + jnp.where(is_control, 1.0, 0.0) * aligned.astype(jnp.float32)
    chosen = jnp.take(captions, caption_ids, axis=0).astype(jnp.float32)
    sequence = jnp.concatenate([chosen, hidden], axis=1)
    modulate = modulation[0]
    normed = (layer_norm(sequence) * (1.0 + modulate[:, 1:2]) + modulate[:, 0:1]).astype(
        jnp.bfloat16
    )
    text_flat = normed.reshape(micro_count * seq_rows, width_full)
    image_flat = normed[:, text_rows:].reshape(flat_rows, width_full)
    local_rows = qkv_weight.shape[1]
    own_cols = lax.dynamic_slice_in_dim(zero_weight, side_index * quarter_width, quarter_width, 1)
    qkv_cols = lax.all_gather(
        qkv_weight[0].reshape(local_rows, 3 * local_heads), "ctl", axis=0, tiled=True
    )
    count_rows = qkv_cols.shape[0]
    packed = jnp.concatenate([out_weight[0].T, own_cols], axis=1)
    spread_out = jnp.broadcast_to(packed[None], (ctl_count,) + packed.shape)
    gathered = lax.all_to_all(spread_out, "ctl", 0, 0, tiled=True).reshape(count_rows, -1)
    query_weight = qkv_cols[:, :local_heads]
    pair_weight = qkv_cols[:, local_heads:]
    out_cols = gathered[:, :local_heads]
    zero_cols = gathered[:, local_heads:]
    query_acc = jnp.dot(image_flat, query_weight, preferred_element_type=jnp.float32)
    pair_acc = jnp.dot(text_flat, pair_weight, preferred_element_type=jnp.float32)
    gain_pair = qk_gain[0]
    queries = head_norm(
        query_acc.reshape(micro_count, img_rows, head_count, HEAD_DIM), gain_pair[0]
    )
    pair_acc = pair_acc.reshape(micro_count, seq_rows, 2, head_count, HEAD_DIM)
    keys_all = head_norm(pair_acc[:, :, 0], gain_pair[1])
    values_all = pair_acc[:, :, 1].astype(jnp.bfloat16)
    scores = jnp.einsum(
        "bihd,bjhd->bhij", queries, keys_all, preferred_element_type=jnp.float32
    ) / math.sqrt(HEAD_DIM)
    attend = jax.nn.softmax(scores, axis=-1).astype(jnp.bfloat16)
    mixed_heads = jnp.einsum(
        "bhij,bjhd->bihd", attend, values_all, preferred_element_type=jnp.float32
    )
    mixed_heads = mixed_heads.astype(jnp.bfloat16).reshape(flat_rows, local_heads)
    contract_last = (((1,), (1,)), ((), ()))
    other_out = lax.dynamic_slice_in_dim(out_cols, (1 - tp_index) * half_width, half_width, 0)
    own_out = lax.dynamic_slice_in_dim(out_cols, tp_index * half_width, half_width, 0)
    other_part = lax.dot_general(
        mixed_heads, other_out, contract_last, preferred_element_type=jnp.float32
    ).astype(jnp.bfloat16)
    got_part = swap(other_part, "tp")
    own_part_heads = rounded(
        lax.dot_general(mixed_heads, own_out, contract_last, preferred_element_type=jnp.float32)
    )
    head_sum = own_part_heads + got_part.astype(jnp.float32)
    hid_half = lax.dynamic_slice_in_dim(hidden, tp_index * half_width, half_width, 2)
    gate_half = lax.dynamic_slice_in_dim(modulate[:, 2:3], tp_index * half_width, half_width, 2)
    act_half = hid_half + gate_half * head_sum.reshape(micro_count, img_rows, half_width)
    act_half = act_half.reshape(flat_rows, half_width)
    act_own = act_half.astype(jnp.bfloat16)
    act_got = swap(act_own, "tp")
    act_narrow = jnp.where(
        tp_index == 0,
        jnp.concatenate([act_own, act_got], axis=1),
        jnp.concatenate([act_got, act_own], axis=1),
    )
    act_other = passed_along(act_narrow, "side", 1)
    control_rows = jnp.where(is_control, act_narrow, act_other)
    own_part = jnp.dot(control_rows, zero_cols, preferred_element_type=jnp.float32)
    own_narrow = own_part.astype(jnp.bfloat16)
    other_narrow = partner(own_narrow, "side", 0)
    residual_narrow = jnp.where(
        is_control,
        jnp.concatenate([own_narrow, other_narrow], axis=1),
        jnp.concatenate([other_narrow, own_narrow], axis=1),
    )
    merged = act_half + residual_narrow.astype(jnp.float32)
    section_out = jnp.where(is_control, residual_narrow, merged.astype(jnp.bfloat16))
    final_half = lax.dynamic_slice_in_dim(final_mod, tp_index * half_width, half_width, 2)
    merged_rows = merged.reshape(micro_count, img_rows, half_width)
    row_total, squares = lax.psum(
        (
            jnp.sum(merged_rows, axis=-1, keepdims=True),
            jnp.sum(merged_rows * merged_rows, axis=-1, keepdims=True),
        ),
        "tp",
    )
    mean_val = row_total / width_full
    spread = squares / width_full - mean_val * mean_val
    scale_inv = lax.rsqrt(spread + EPS)
    unit_rows = (merged_rows - mean_val) * scale_inv
    final_in = (unit_rows * (1.0 + final_half[:, 1:2]) + final_half[:, 0:1]).astype(jnp.bfloat16)
    pred_part = jnp.dot(
        final_in.reshape(flat_rows, half_width), proj_weight, preferred_element_type=jnp.float32
    )
    prediction = pred_part + swap(pred_part, "tp")
    loss_factor = 4.0 / math.sqrt(micro_count * ctl_count * img_rows)
    grad_pred = (loss_factor * (prediction - velocity_target.reshape(flat_rows, -1))).astype(
        jnp.bfloat16
    )
    grad_unit = lax.dot_general(
        grad_pred, proj_weight, (((1,), (1,)), ((), ())), preferred_element_type=jnp.float32
    )
    grad_unit = grad_unit.reshape(micro_count, img_rows, half_width) * (1.0 + final_half[:, 1:2])
    first_sum, second_sum = lax.psum(
        (
            jnp.sum(grad_unit, axis=-1, keepdims=True),
            jnp.sum(grad_unit * unit_rows, axis=-1, keepdims=True),
        ),
        "tp",
    )
    grad_narrow = (
        (grad_unit - first_sum / width_full - unit_rows * (second_sum / width_full)) * scale_inv
    ).astype(jnp.bfloat16)
    grad_narrow = grad_narrow.reshape(flat_rows, half_width)
    returned = passed_along(grad_narrow, "side", -1)
    grad_rows_all = jnp.where(is_control, returned, grad_narrow)
    own_act = lax.dynamic_index_in_dim(
        control_rows.reshape(flat_rows, ctl_count, 2, block_rows), side_index, 2, keepdims=False
    )
    own_act = own_act.reshape(flat_rows, ctl_count * block_rows)
    product = lax.dot_general(
        own_act, grad_rows_all, (((0,), (0,)), ((), ())), preferred_element_type=jnp.float32
    )
    group_parts = rounded(product).astype(jnp.bfloat16).reshape(ctl_count, block_rows, half_width)
    received = lax.all_to_all(group_parts, "ctl", 0, 0, tiled=True)
    zero_grad = jnp.sum(received.astype(jnp.float32), axis=0)
    return (section_out.reshape(1, micro_count, img_rows, half_width), zero_grad)


def solution(mesh):
    return jax.shard_map(
        local,
        mesh=mesh,
        in_specs=(
            P("ctl", None, None),
            P("ctl", None, None),
            P("ctl", None),
            P("ctl", None, None),
            P("ctl"),
            P("side", "ctl", None, None),
            P("side", "ctl", None, "tp"),
            P("side", None, None),
            P("side", "tp", "ctl"),
            P("ctl", "tp"),
            P("tp", None),
            P("ctl", None, None),
            P("ctl", None, None),
        ),
        out_specs=(P("side", "ctl", None, "tp"), P(("ctl", "side"), "tp")),
        check_vma=False,
    )
```

```python
import math

import jax
import jax.numpy as jnp
from jax import lax
from jax.experimental import pallas as pl
from jax.sharding import PartitionSpec as P

HEAD_DIM = 128


EPS = 1e-06


def passed_along(shard, axis, by):
    length = lax.axis_size(axis)
    pairs = [(i, i + by) for i in range(length) if 0 <= i + by < length]
    return lax.ppermute(shard, axis, pairs)


def partner(value, axis, bit):
    mask = 2**bit
    pairs = [(source, source ^ mask) for source in range(lax.axis_size(axis))]
    return lax.ppermute(value, axis, pairs)


def swap(value, axis):
    return lax.ppermute(value, axis, [(0, 1), (1, 0)])


def block_matmul(rows, weight, first_block, block_count, width):
    row_count, depth = rows.shape

    def kernel(rows_ref, weight_ref, out_ref):
        out_ref[...] = jnp.dot(rows_ref[...], weight_ref[...], preferred_element_type=jnp.float32)

    return pl.pallas_call(
        kernel,
        grid=(block_count,),
        in_specs=[
            pl.BlockSpec((row_count, depth), lambda n: (0, 0)),
            pl.BlockSpec((depth, width), lambda n: (0, first_block + n)),
        ],
        out_specs=pl.BlockSpec((row_count, width), lambda n: (0, n)),
        out_shape=jax.ShapeDtypeStruct((row_count, block_count * width), jnp.float32),
        cost_estimate=pl.CostEstimate(
            flops=2 * row_count * depth * block_count * width,
            transcendentals=0,
            bytes_accessed=2 * depth * (row_count + block_count * width)
            + 4 * row_count * block_count * width,
        ),
    )(rows, weight)


def layer_norm(values):
    center = values - jnp.mean(values, axis=-1, keepdims=True)
    spread = jnp.mean(center * center, axis=-1, keepdims=True)
    return center * lax.rsqrt(spread + EPS)


def head_norm(values, gain_row):
    power_mean = jnp.mean(values * values, axis=-1, keepdims=True)
    return (values * lax.rsqrt(power_mean + EPS) * gain_row).astype(jnp.bfloat16)


def rounded(values):
    narrow = lax.optimization_barrier(values.astype(jnp.bfloat16))
    return narrow.astype(jnp.float32)


def local(
    image_latent,
    control_latent,
    control_order,
    captions,
    caption_ids,
    modulation,
    qkv_weight,
    qk_gain,
    out_weight,
    zero_weight,
    proj_weight,
    final_mod,
    velocity_target,
):
    side_index = lax.axis_index("side")
    tp_index = lax.axis_index("tp")
    ctl_count = lax.axis_size("ctl")
    tp_count = lax.axis_size("tp")
    is_control = side_index == 0
    micro_count, img_rows, width_full = image_latent.shape
    text_rows = captions.shape[1]
    seq_rows = text_rows + img_rows
    local_heads = qkv_weight.shape[3]
    head_count = local_heads // HEAD_DIM
    half_width = width_full // tp_count
    quarter_width = half_width // 2
    flat_rows = micro_count * img_rows
    block_rows = width_full // (2 * ctl_count)
    aligned = jax.vmap(lambda latent, order_row: jnp.take(latent, order_row, axis=0))(
        control_latent, control_order
    )
    plain_rows = image_latent.astype(jnp.float32)
    hidden = plain_rows + jnp.where(is_control, 1.0, 0.0) * aligned.astype(jnp.float32)
    chosen = jnp.take(captions, caption_ids, axis=0).astype(jnp.float32)
    sequence = jnp.concatenate([chosen, hidden], axis=1)
    modulate = modulation[0]
    normed = (layer_norm(sequence) * (1.0 + modulate[:, 1:2]) + modulate[:, 0:1]).astype(
        jnp.bfloat16
    )
    text_flat = normed.reshape(micro_count * seq_rows, width_full)
    image_flat = normed[:, text_rows:].reshape(flat_rows, width_full)
    local_rows = qkv_weight.shape[1]
    own_cols = lax.dynamic_slice_in_dim(zero_weight, side_index * quarter_width, quarter_width, 1)
    packed = jnp.concatenate(
        [
            qkv_weight[0].reshape(local_rows, 3 * local_heads),
            out_weight[0].T,
            own_cols,
        ],
        axis=1,
    )
    gathered = lax.all_gather(packed, "ctl", axis=0, tiled=True)
    count_rows = gathered.shape[0]
    out_cols = gathered[:, 3 * local_heads : 4 * local_heads]
    projected = block_matmul(text_flat, gathered, 0, 3, local_heads)
    projected = projected.reshape(micro_count, seq_rows, 3 * local_heads)
    query_acc = projected[:, text_rows:, :local_heads]
    pair_acc = projected[:, :, local_heads:]
    gain_pair = qk_gain[0]
    queries = head_norm(
        query_acc.reshape(micro_count, img_rows, head_count, HEAD_DIM), gain_pair[0]
    )
    pair_acc = pair_acc.reshape(micro_count, seq_rows, 2, head_count, HEAD_DIM)
    keys_all = head_norm(pair_acc[:, :, 0], gain_pair[1])
    values_all = pair_acc[:, :, 1].astype(jnp.bfloat16)
    scores = jnp.einsum(
        "bihd,bjhd->bhij", queries, keys_all, preferred_element_type=jnp.float32
    ) / math.sqrt(HEAD_DIM)
    attend = jax.nn.softmax(scores, axis=-1).astype(jnp.bfloat16)
    mixed_heads = jnp.einsum(
        "bhij,bjhd->bihd", attend, values_all, preferred_element_type=jnp.float32
    )
    mixed_heads = mixed_heads.astype(jnp.bfloat16).reshape(flat_rows, local_heads)
    contract_last = (((1,), (1,)), ((), ()))
    other_out = lax.dynamic_slice_in_dim(out_cols, (1 - tp_index) * half_width, half_width, 0)
    own_out = lax.dynamic_slice_in_dim(out_cols, tp_index * half_width, half_width, 0)
    other_part = lax.dot_general(
        mixed_heads, other_out, contract_last, preferred_element_type=jnp.float32
    ).astype(jnp.bfloat16)
    got_part = swap(other_part, "tp")
    own_part_heads = rounded(
        lax.dot_general(mixed_heads, own_out, contract_last, preferred_element_type=jnp.float32)
    )
    head_sum = own_part_heads + got_part.astype(jnp.float32)
    hid_half = lax.dynamic_slice_in_dim(hidden, tp_index * half_width, half_width, 2)
    gate_half = lax.dynamic_slice_in_dim(modulate[:, 2:3], tp_index * half_width, half_width, 2)
    act_half = hid_half + gate_half * head_sum.reshape(micro_count, img_rows, half_width)
    act_half = act_half.reshape(flat_rows, half_width)
    act_own = act_half.astype(jnp.bfloat16)
    act_got = swap(act_own, "tp")
    act_narrow = jnp.where(
        tp_index == 0,
        jnp.concatenate([act_own, act_got], axis=1),
        jnp.concatenate([act_got, act_own], axis=1),
    )
    act_other = passed_along(act_narrow, "side", 1)
    control_rows = jnp.where(is_control, act_narrow, act_other)
    own_part = block_matmul(control_rows, gathered, 4, 1, local_heads)
    own_narrow = own_part.astype(jnp.bfloat16)
    other_narrow = partner(own_narrow, "side", 0)
    residual_narrow = jnp.where(
        is_control,
        jnp.concatenate([own_narrow, other_narrow], axis=1),
        jnp.concatenate([other_narrow, own_narrow], axis=1),
    )
    merged = act_half + residual_narrow.astype(jnp.float32)
    section_out = jnp.where(is_control, residual_narrow, merged.astype(jnp.bfloat16))
    final_half = lax.dynamic_slice_in_dim(final_mod, tp_index * half_width, half_width, 2)
    merged_rows = merged.reshape(micro_count, img_rows, half_width)
    row_total, squares = lax.psum(
        (
            jnp.sum(merged_rows, axis=-1, keepdims=True),
            jnp.sum(merged_rows * merged_rows, axis=-1, keepdims=True),
        ),
        "tp",
    )
    mean_val = row_total / width_full
    spread = squares / width_full - mean_val * mean_val
    scale_inv = lax.rsqrt(spread + EPS)
    unit_rows = (merged_rows - mean_val) * scale_inv
    final_in = (unit_rows * (1.0 + final_half[:, 1:2]) + final_half[:, 0:1]).astype(jnp.bfloat16)
    pred_part = jnp.dot(
        final_in.reshape(flat_rows, half_width), proj_weight, preferred_element_type=jnp.float32
    )
    prediction = pred_part + swap(pred_part, "tp")
    loss_factor = 4.0 / math.sqrt(micro_count * ctl_count * img_rows)
    grad_pred = (loss_factor * (prediction - velocity_target.reshape(flat_rows, -1))).astype(
        jnp.bfloat16
    )
    grad_unit = lax.dot_general(
        grad_pred, proj_weight, (((1,), (1,)), ((), ())), preferred_element_type=jnp.float32
    )
    grad_unit = grad_unit.reshape(micro_count, img_rows, half_width) * (1.0 + final_half[:, 1:2])
    first_sum, second_sum = lax.psum(
        (
            jnp.sum(grad_unit, axis=-1, keepdims=True),
            jnp.sum(grad_unit * unit_rows, axis=-1, keepdims=True),
        ),
        "tp",
    )
    grad_narrow = (
        (grad_unit - first_sum / width_full - unit_rows * (second_sum / width_full)) * scale_inv
    ).astype(jnp.bfloat16)
    grad_narrow = grad_narrow.reshape(flat_rows, half_width)
    returned = passed_along(grad_narrow, "side", -1)
    grad_rows_all = jnp.where(is_control, returned, grad_narrow)
    own_act = lax.dynamic_index_in_dim(
        control_rows.reshape(flat_rows, ctl_count, 2, block_rows), side_index, 2, keepdims=False
    )
    own_act = own_act.reshape(flat_rows, ctl_count * block_rows)
    product = lax.dot_general(
        own_act, grad_rows_all, (((0,), (0,)), ((), ())), preferred_element_type=jnp.float32
    )
    group_parts = rounded(product).astype(jnp.bfloat16).reshape(ctl_count, block_rows, half_width)
    received = lax.all_to_all(group_parts, "ctl", 0, 0, tiled=True)
    zero_grad = jnp.sum(received.astype(jnp.float32), axis=0)
    return (section_out.reshape(1, micro_count, img_rows, half_width), zero_grad)


def solution(mesh):
    return jax.shard_map(
        local,
        mesh=mesh,
        in_specs=(
            P("ctl", None, None),
            P("ctl", None, None),
            P("ctl", None),
            P("ctl", None, None),
            P("ctl"),
            P("side", "ctl", None, None),
            P("side", "ctl", None, "tp"),
            P("side", None, None),
            P("side", "tp", "ctl"),
            P("ctl", "tp"),
            P("tp", None),
            P("ctl", None, None),
            P("ctl", None, None),
        ),
        out_specs=(P("side", "ctl", None, "tp"), P(("ctl", "side"), "tp")),
        check_vma=False,
    )
```

```python
import math

import jax
import jax.numpy as jnp
from jax import lax
from jax.experimental import pallas as pl
from jax.sharding import PartitionSpec as P

HEAD_DIM = 128


EPS = 1e-06


def passed_along(shard, axis, by):
    length = lax.axis_size(axis)
    pairs = [(i, i + by) for i in range(length) if 0 <= i + by < length]
    return lax.ppermute(shard, axis, pairs)


def partner(value, axis, bit):
    mask = 2**bit
    pairs = [(source, source ^ mask) for source in range(lax.axis_size(axis))]
    return lax.ppermute(value, axis, pairs)


def swap(value, axis):
    return lax.ppermute(value, axis, [(0, 1), (1, 0)])


def block_matmul(rows, weight, first_block, block_count, width):
    row_count, depth = rows.shape

    def kernel(rows_ref, weight_ref, out_ref):
        out_ref[...] = jnp.dot(rows_ref[...], weight_ref[...], preferred_element_type=jnp.float32)

    return pl.pallas_call(
        kernel,
        grid=(block_count,),
        in_specs=[
            pl.BlockSpec((row_count, depth), lambda n: (0, 0)),
            pl.BlockSpec((depth, width), lambda n: (0, first_block + n)),
        ],
        out_specs=pl.BlockSpec((row_count, width), lambda n: (0, n)),
        out_shape=jax.ShapeDtypeStruct((row_count, block_count * width), jnp.float32),
        cost_estimate=pl.CostEstimate(
            flops=2 * row_count * depth * block_count * width,
            transcendentals=0,
            bytes_accessed=2 * depth * (row_count + block_count * width)
            + 4 * row_count * block_count * width,
        ),
    )(rows, weight)


def layer_norm(values):
    center = values - jnp.mean(values, axis=-1, keepdims=True)
    spread = jnp.mean(center * center, axis=-1, keepdims=True)
    return center * lax.rsqrt(spread + EPS)


def head_norm(values, gain_row):
    power_mean = jnp.mean(values * values, axis=-1, keepdims=True)
    return (values * lax.rsqrt(power_mean + EPS) * gain_row).astype(jnp.bfloat16)


def rounded(values):
    narrow = lax.optimization_barrier(values.astype(jnp.bfloat16))
    return narrow.astype(jnp.float32)


def local(
    image_latent,
    control_latent,
    control_order,
    captions,
    caption_ids,
    modulation,
    qkv_weight,
    qk_gain,
    out_weight,
    zero_weight,
    proj_weight,
    final_mod,
    velocity_target,
):
    side_index = lax.axis_index("side")
    tp_index = lax.axis_index("tp")
    ctl_count = lax.axis_size("ctl")
    tp_count = lax.axis_size("tp")
    is_control = side_index == 0
    micro_count, img_rows, width_full = image_latent.shape
    text_rows = captions.shape[1]
    seq_rows = text_rows + img_rows
    local_heads = qkv_weight.shape[3]
    head_count = local_heads // HEAD_DIM
    half_width = width_full // tp_count
    quarter_width = half_width // 2
    flat_rows = micro_count * img_rows
    block_rows = width_full // (2 * ctl_count)
    aligned = jax.vmap(lambda latent, order_row: jnp.take(latent, order_row, axis=0))(
        control_latent, control_order
    )
    plain_rows = image_latent.astype(jnp.float32)
    hidden = plain_rows + jnp.where(is_control, 1.0, 0.0) * aligned.astype(jnp.float32)
    chosen = jnp.take(captions, caption_ids, axis=0).astype(jnp.float32)
    sequence = jnp.concatenate([chosen, hidden], axis=1)
    modulate = modulation[0]
    normed = (layer_norm(sequence) * (1.0 + modulate[:, 1:2]) + modulate[:, 0:1]).astype(
        jnp.bfloat16
    )
    text_flat = normed.reshape(micro_count * seq_rows, width_full)
    image_flat = normed[:, text_rows:].reshape(flat_rows, width_full)
    local_rows = qkv_weight.shape[1]
    own_cols = lax.dynamic_slice_in_dim(zero_weight, side_index * quarter_width, quarter_width, 1)
    packed = jnp.concatenate(
        [
            qkv_weight[0].reshape(local_rows, 3 * local_heads),
            out_weight[0].T,
            own_cols,
        ],
        axis=1,
    )
    gathered = lax.all_gather(packed, "ctl", axis=0, tiled=True)
    count_rows = gathered.shape[0]
    out_cols = gathered[:, 3 * local_heads : 4 * local_heads]
    projected = block_matmul(text_flat, gathered, 0, 3, local_heads)
    projected = projected.reshape(micro_count, seq_rows, 3 * local_heads)
    query_acc = projected[:, text_rows:, :local_heads]
    pair_acc = projected[:, :, local_heads:]
    gain_pair = qk_gain[0]
    contract_last = (((1,), (1,)), ((), ()))
    other_out = lax.dynamic_slice_in_dim(out_cols, (1 - tp_index) * half_width, half_width, 0)
    own_out = lax.dynamic_slice_in_dim(out_cols, tp_index * half_width, half_width, 0)
    hid_half = lax.dynamic_slice_in_dim(hidden, tp_index * half_width, half_width, 2)
    gate_half = lax.dynamic_slice_in_dim(modulate[:, 2:3], tp_index * half_width, half_width, 2)
    act_halves = []
    act_rows = []
    for sample in range(micro_count):
        queries = head_norm(
            query_acc[sample].reshape(img_rows, head_count, HEAD_DIM), gain_pair[0]
        )
        pair_one = pair_acc[sample].reshape(seq_rows, 2, head_count, HEAD_DIM)
        keys_all = head_norm(pair_one[:, 0], gain_pair[1])
        values_all = pair_one[:, 1].astype(jnp.bfloat16)
        scores = jnp.einsum(
            "ihd,jhd->hij", queries, keys_all, preferred_element_type=jnp.float32
        ) / math.sqrt(HEAD_DIM)
        attend = jax.nn.softmax(scores, axis=-1).astype(jnp.bfloat16)
        mixed_heads = jnp.einsum(
            "hij,jhd->ihd", attend, values_all, preferred_element_type=jnp.float32
        )
        mixed_heads = mixed_heads.astype(jnp.bfloat16).reshape(img_rows, local_heads)
        other_part = lax.dot_general(
            mixed_heads, other_out, contract_last, preferred_element_type=jnp.float32
        ).astype(jnp.bfloat16)
        got_part = swap(other_part, "tp")
        own_part_heads = rounded(
            lax.dot_general(mixed_heads, own_out, contract_last, preferred_element_type=jnp.float32)
        )
        head_sum = own_part_heads + got_part.astype(jnp.float32)
        act_one = hid_half[sample] + gate_half[sample] * head_sum
        act_own = act_one.astype(jnp.bfloat16)
        act_got = swap(act_own, "tp")
        act_halves.append(act_one)
        act_rows.append(
            jnp.where(
                tp_index == 0,
                jnp.concatenate([act_own, act_got], axis=1),
                jnp.concatenate([act_got, act_own], axis=1),
            )
        )
    act_half = jnp.concatenate(act_halves, axis=0)
    act_narrow = jnp.concatenate(act_rows, axis=0)
    act_other = passed_along(act_narrow, "side", 1)
    control_rows = jnp.where(is_control, act_narrow, act_other)
    own_part = block_matmul(control_rows, gathered, 4, 1, local_heads)
    own_narrow = own_part.astype(jnp.bfloat16)
    other_narrow = partner(own_narrow, "side", 0)
    residual_narrow = jnp.where(
        is_control,
        jnp.concatenate([own_narrow, other_narrow], axis=1),
        jnp.concatenate([other_narrow, own_narrow], axis=1),
    )
    merged = act_half + residual_narrow.astype(jnp.float32)
    section_out = jnp.where(is_control, residual_narrow, merged.astype(jnp.bfloat16))
    final_half = lax.dynamic_slice_in_dim(final_mod, tp_index * half_width, half_width, 2)
    merged_rows = merged.reshape(micro_count, img_rows, half_width)
    row_total, squares = lax.psum(
        (
            jnp.sum(merged_rows, axis=-1, keepdims=True),
            jnp.sum(merged_rows * merged_rows, axis=-1, keepdims=True),
        ),
        "tp",
    )
    mean_val = row_total / width_full
    spread = squares / width_full - mean_val * mean_val
    scale_inv = lax.rsqrt(spread + EPS)
    unit_rows = (merged_rows - mean_val) * scale_inv
    final_in = (unit_rows * (1.0 + final_half[:, 1:2]) + final_half[:, 0:1]).astype(jnp.bfloat16)
    pred_part = jnp.dot(
        final_in.reshape(flat_rows, half_width), proj_weight, preferred_element_type=jnp.float32
    )
    prediction = pred_part + swap(pred_part, "tp")
    loss_factor = 4.0 / math.sqrt(micro_count * ctl_count * img_rows)
    grad_pred = (loss_factor * (prediction - velocity_target.reshape(flat_rows, -1))).astype(
        jnp.bfloat16
    )
    grad_unit = lax.dot_general(
        grad_pred, proj_weight, (((1,), (1,)), ((), ())), preferred_element_type=jnp.float32
    )
    grad_unit = grad_unit.reshape(micro_count, img_rows, half_width) * (1.0 + final_half[:, 1:2])
    first_sum, second_sum = lax.psum(
        (
            jnp.sum(grad_unit, axis=-1, keepdims=True),
            jnp.sum(grad_unit * unit_rows, axis=-1, keepdims=True),
        ),
        "tp",
    )
    grad_narrow = (
        (grad_unit - first_sum / width_full - unit_rows * (second_sum / width_full)) * scale_inv
    ).astype(jnp.bfloat16)
    grad_narrow = grad_narrow.reshape(flat_rows, half_width)
    returned = passed_along(grad_narrow, "side", -1)
    grad_rows_all = jnp.where(is_control, returned, grad_narrow)
    own_act = lax.dynamic_index_in_dim(
        control_rows.reshape(flat_rows, ctl_count, 2, block_rows), side_index, 2, keepdims=False
    )
    own_act = own_act.reshape(flat_rows, ctl_count * block_rows)
    product = lax.dot_general(
        own_act, grad_rows_all, (((0,), (0,)), ((), ())), preferred_element_type=jnp.float32
    )
    group_parts = rounded(product).astype(jnp.bfloat16).reshape(ctl_count, block_rows, half_width)
    received = lax.all_to_all(group_parts, "ctl", 0, 0, tiled=True)
    zero_grad = jnp.sum(received.astype(jnp.float32), axis=0)
    return (section_out.reshape(1, micro_count, img_rows, half_width), zero_grad)


def solution(mesh):
    return jax.shard_map(
        local,
        mesh=mesh,
        in_specs=(
            P("ctl", None, None),
            P("ctl", None, None),
            P("ctl", None),
            P("ctl", None, None),
            P("ctl"),
            P("side", "ctl", None, None),
            P("side", "ctl", None, "tp"),
            P("side", None, None),
            P("side", "tp", "ctl"),
            P("ctl", "tp"),
            P("tp", None),
            P("ctl", None, None),
            P("ctl", None, None),
        ),
        out_specs=(P("side", "ctl", None, "tp"), P(("ctl", "side"), "tp")),
        check_vma=False,
    )
```

```python
import math

import jax
import jax.numpy as jnp
from jax import lax
from jax.experimental import pallas as pl
from jax.sharding import PartitionSpec as P

HEAD_DIM = 128


EPS = 1e-06


def passed_along(shard, axis, by):
    length = lax.axis_size(axis)
    pairs = [(i, i + by) for i in range(length) if 0 <= i + by < length]
    return lax.ppermute(shard, axis, pairs)


def partner(value, axis, bit):
    mask = 2**bit
    pairs = [(source, source ^ mask) for source in range(lax.axis_size(axis))]
    return lax.ppermute(value, axis, pairs)


def swap(value, axis):
    return lax.ppermute(value, axis, [(0, 1), (1, 0)])


def block_matmul(rows, weight, first_block, block_count, width):
    row_count, depth = rows.shape

    def kernel(rows_ref, weight_ref, out_ref):
        out_ref[...] = jnp.dot(rows_ref[...], weight_ref[...], preferred_element_type=jnp.float32)

    return pl.pallas_call(
        kernel,
        grid=(block_count,),
        in_specs=[
            pl.BlockSpec((row_count, depth), lambda n: (0, 0)),
            pl.BlockSpec((depth, width), lambda n: (0, first_block + n)),
        ],
        out_specs=pl.BlockSpec((row_count, width), lambda n: (0, n)),
        out_shape=jax.ShapeDtypeStruct((row_count, block_count * width), jnp.float32),
        cost_estimate=pl.CostEstimate(
            flops=2 * row_count * depth * block_count * width,
            transcendentals=0,
            bytes_accessed=2 * depth * (row_count + block_count * width)
            + 4 * row_count * block_count * width,
        ),
    )(rows, weight)


def layer_norm(values):
    center = values - jnp.mean(values, axis=-1, keepdims=True)
    spread = jnp.mean(center * center, axis=-1, keepdims=True)
    return center * lax.rsqrt(spread + EPS)


def head_norm(values, gain_row):
    power_mean = jnp.mean(values * values, axis=-1, keepdims=True)
    return (values * lax.rsqrt(power_mean + EPS) * gain_row).astype(jnp.bfloat16)


def rounded(values):
    narrow = lax.optimization_barrier(values.astype(jnp.bfloat16))
    return narrow.astype(jnp.float32)


def local(
    image_latent,
    control_latent,
    control_order,
    captions,
    caption_ids,
    modulation,
    qkv_weight,
    qk_gain,
    out_weight,
    zero_weight,
    proj_weight,
    final_mod,
    velocity_target,
):
    side_index = lax.axis_index("side")
    tp_index = lax.axis_index("tp")
    ctl_count = lax.axis_size("ctl")
    tp_count = lax.axis_size("tp")
    is_control = side_index == 0
    micro_count, img_rows, width_full = image_latent.shape
    text_rows = captions.shape[1]
    seq_rows = text_rows + img_rows
    local_heads = qkv_weight.shape[3]
    head_count = local_heads // HEAD_DIM
    half_width = width_full // tp_count
    quarter_width = half_width // 2
    flat_rows = micro_count * img_rows
    block_rows = width_full // (2 * ctl_count)
    aligned = jax.vmap(lambda latent, order_row: jnp.take(latent, order_row, axis=0))(
        control_latent, control_order
    )
    plain_rows = image_latent.astype(jnp.float32)
    hidden = plain_rows + jnp.where(is_control, 1.0, 0.0) * aligned.astype(jnp.float32)
    chosen = jnp.take(captions, caption_ids, axis=0).astype(jnp.float32)
    sequence = jnp.concatenate([chosen, hidden], axis=1)
    modulate = modulation[0]
    normed = (layer_norm(sequence) * (1.0 + modulate[:, 1:2]) + modulate[:, 0:1]).astype(
        jnp.bfloat16
    )
    text_flat = normed.reshape(micro_count * seq_rows, width_full)
    image_flat = normed[:, text_rows:].reshape(flat_rows, width_full)
    local_rows = qkv_weight.shape[1]
    own_cols = lax.dynamic_slice_in_dim(zero_weight, side_index * quarter_width, quarter_width, 1)
    packed = jnp.concatenate(
        [
            qkv_weight[0].reshape(local_rows, 3 * local_heads),
            out_weight[0].T,
            own_cols,
        ],
        axis=1,
    )
    gathered = lax.all_gather(packed, "ctl", axis=0, tiled=True)
    count_rows = gathered.shape[0]
    out_cols = gathered[:, 3 * local_heads : 4 * local_heads]
    projected = block_matmul(text_flat, gathered, 0, 3, local_heads)
    projected = projected.reshape(micro_count, seq_rows, 3 * local_heads)
    query_acc = projected[:, text_rows:, :local_heads]
    pair_acc = projected[:, :, local_heads:]
    gain_pair = qk_gain[0]
    contract_last = (((1,), (1,)), ((), ()))
    other_out = lax.dynamic_slice_in_dim(out_cols, (1 - tp_index) * half_width, half_width, 0)
    own_out = lax.dynamic_slice_in_dim(out_cols, tp_index * half_width, half_width, 0)
    hid_half = lax.dynamic_slice_in_dim(hidden, tp_index * half_width, half_width, 2)
    gate_half = lax.dynamic_slice_in_dim(modulate[:, 2:3], tp_index * half_width, half_width, 2)
    act_halves = []
    act_rows = []
    for sample in range(micro_count):
        queries = head_norm(
            query_acc[sample].reshape(img_rows, head_count, HEAD_DIM), gain_pair[0]
        )
        pair_one = pair_acc[sample].reshape(seq_rows, 2, head_count, HEAD_DIM)
        keys_all = head_norm(pair_one[:, 0], gain_pair[1])
        values_all = pair_one[:, 1].astype(jnp.bfloat16)
        scores = jnp.einsum(
            "ihd,jhd->hij", queries, keys_all, preferred_element_type=jnp.float32
        ) / math.sqrt(HEAD_DIM)
        attend = jax.nn.softmax(scores, axis=-1).astype(jnp.bfloat16)
        mixed_heads = jnp.einsum(
            "hij,jhd->ihd", attend, values_all, preferred_element_type=jnp.float32
        )
        mixed_heads = mixed_heads.astype(jnp.bfloat16).reshape(img_rows, local_heads)
        other_part = lax.dot_general(
            mixed_heads, other_out, contract_last, preferred_element_type=jnp.float32
        ).astype(jnp.bfloat16)
        got_part = swap(other_part, "tp")
        own_part_heads = rounded(
            lax.dot_general(mixed_heads, own_out, contract_last, preferred_element_type=jnp.float32)
        )
        head_sum = own_part_heads + got_part.astype(jnp.float32)
        act_one = hid_half[sample] + gate_half[sample] * head_sum
        act_own = act_one.astype(jnp.bfloat16)
        act_got = lax.ppermute(act_own, ("side", "tp"), [(0, 1), (1, 0)])
        act_halves.append(act_one)
        act_rows.append(
            jnp.where(
                tp_index == 0,
                jnp.concatenate([act_own, act_got], axis=1),
                jnp.concatenate([act_got, act_own], axis=1),
            )
        )
    act_half = jnp.concatenate(act_halves, axis=0)
    act_narrow = jnp.concatenate(act_rows, axis=0)
    act_other = passed_along(act_narrow, "side", 1)
    control_rows = jnp.where(is_control, act_narrow, act_other)
    own_part = block_matmul(control_rows, gathered, 4, 1, local_heads)
    own_narrow = own_part.astype(jnp.bfloat16)
    other_narrow = partner(own_narrow, "side", 0)
    residual_narrow = jnp.where(
        is_control,
        jnp.concatenate([own_narrow, other_narrow], axis=1),
        jnp.concatenate([other_narrow, own_narrow], axis=1),
    )
    merged = act_half + residual_narrow.astype(jnp.float32)
    section_out = jnp.where(is_control, residual_narrow, merged.astype(jnp.bfloat16))
    final_half = lax.dynamic_slice_in_dim(final_mod, tp_index * half_width, half_width, 2)
    merged_rows = merged.reshape(micro_count, img_rows, half_width)
    row_total, squares = lax.psum(
        (
            jnp.sum(merged_rows, axis=-1, keepdims=True),
            jnp.sum(merged_rows * merged_rows, axis=-1, keepdims=True),
        ),
        "tp",
    )
    mean_val = row_total / width_full
    spread = squares / width_full - mean_val * mean_val
    scale_inv = lax.rsqrt(spread + EPS)
    unit_rows = (merged_rows - mean_val) * scale_inv
    final_in = (unit_rows * (1.0 + final_half[:, 1:2]) + final_half[:, 0:1]).astype(jnp.bfloat16)
    pred_part = jnp.dot(
        final_in.reshape(flat_rows, half_width), proj_weight, preferred_element_type=jnp.float32
    )
    prediction = pred_part + swap(pred_part, "tp")
    loss_factor = 4.0 / math.sqrt(micro_count * ctl_count * img_rows)
    grad_pred = (loss_factor * (prediction - velocity_target.reshape(flat_rows, -1))).astype(
        jnp.bfloat16
    )
    grad_unit = lax.dot_general(
        grad_pred, proj_weight, (((1,), (1,)), ((), ())), preferred_element_type=jnp.float32
    )
    grad_unit = grad_unit.reshape(micro_count, img_rows, half_width) * (1.0 + final_half[:, 1:2])
    first_sum, second_sum = lax.psum(
        (
            jnp.sum(grad_unit, axis=-1, keepdims=True),
            jnp.sum(grad_unit * unit_rows, axis=-1, keepdims=True),
        ),
        "tp",
    )
    grad_narrow = (
        (grad_unit - first_sum / width_full - unit_rows * (second_sum / width_full)) * scale_inv
    ).astype(jnp.bfloat16)
    grad_narrow = grad_narrow.reshape(flat_rows, half_width)
    returned = passed_along(grad_narrow, "side", -1)
    grad_rows_all = jnp.where(is_control, returned, grad_narrow)
    own_act = lax.dynamic_index_in_dim(
        control_rows.reshape(flat_rows, ctl_count, 2, block_rows), side_index, 2, keepdims=False
    )
    own_act = own_act.reshape(flat_rows, ctl_count * block_rows)
    product = lax.dot_general(
        own_act, grad_rows_all, (((0,), (0,)), ((), ())), preferred_element_type=jnp.float32
    )
    group_parts = rounded(product).astype(jnp.bfloat16).reshape(ctl_count, block_rows, half_width)
    received = lax.all_to_all(group_parts, "ctl", 0, 0, tiled=True)
    zero_grad = jnp.sum(received.astype(jnp.float32), axis=0)
    return (section_out.reshape(1, micro_count, img_rows, half_width), zero_grad)


def solution(mesh):
    return jax.shard_map(
        local,
        mesh=mesh,
        in_specs=(
            P("ctl", None, None),
            P("ctl", None, None),
            P("ctl", None),
            P("ctl", None, None),
            P("ctl"),
            P("side", "ctl", None, None),
            P("side", "ctl", None, "tp"),
            P("side", None, None),
            P("side", "tp", "ctl"),
            P("ctl", "tp"),
            P("tp", None),
            P("ctl", None, None),
            P("ctl", None, None),
        ),
        out_specs=(P("side", "ctl", None, "tp"), P(("ctl", "side"), "tp")),
        check_vma=False,
    )
```

```python
import math

import jax
import jax.numpy as jnp
from jax import lax
from jax.experimental import pallas as pl
from jax.sharding import PartitionSpec as P

HEAD_DIM = 128


EPS = 1e-06


def passed_along(shard, axis, by):
    length = lax.axis_size(axis)
    pairs = [(i, i + by) for i in range(length) if 0 <= i + by < length]
    return lax.ppermute(shard, axis, pairs)


def partner(value, axis, bit):
    mask = 2**bit
    pairs = [(source, source ^ mask) for source in range(lax.axis_size(axis))]
    return lax.ppermute(value, axis, pairs)


CTL_SHAPE = (4, 2, 4)


def ctl_coords(index):
    _, count_z, count_x = CTL_SHAPE
    return index // (count_z * count_x), (index // count_x) % count_z, index % count_x


def ctl_shift(value, step_y, flip_z, step_x):
    count_y, count_z, count_x = CTL_SHAPE
    pairs = []
    for source in range(count_y * count_z * count_x):
        at_y, at_z, at_x = ctl_coords(source)
        target = ((at_y + step_y) % count_y * count_z + (at_z ^ flip_z)) * count_x + (at_x + step_x) % count_x
        pairs.append((source, target))
    return lax.ppermute(value, "ctl", pairs)


def ring_stage(block, along_y, position):
    step = (1, 0) if along_y else (0, 1)
    forward = lambda value: ctl_shift(value, step[0], 0, step[1])
    backward = lambda value: ctl_shift(value, -step[0], 0, -step[1])
    from_before = forward(block)
    from_after = backward(block)
    half = block.shape[0] // 2
    far = jnp.concatenate([backward(from_after[:half]), forward(from_before[half:])], axis=0)
    relative = jnp.stack([block, from_after, far, from_before])
    return jnp.roll(relative, position, axis=0)


def ctl_gather(piece):
    at_y, at_z, at_x = ctl_coords(lax.axis_index("ctl"))
    rows, width = piece.shape
    paired = ctl_shift(piece, 0, 1, 0)
    pair = jnp.where(at_z == 0, jnp.stack([piece, paired]), jnp.stack([paired, piece]))
    split = width // 2
    first = ring_stage(pair[..., :split], False, at_x)
    first = ring_stage(jnp.swapaxes(first, 0, 1), True, at_y)
    second = ring_stage(pair[..., split:], True, at_y)
    second = ring_stage(second, False, at_x)
    second = jnp.moveaxis(second, 0, 2)
    return jnp.concatenate(
        [first.reshape(-1, split), second.reshape(-1, width - split)], axis=1
    )


def swap(value, axis):
    return lax.ppermute(value, axis, [(0, 1), (1, 0)])


def block_matmul(rows, weight, first_block, block_count, width):
    row_count, depth = rows.shape

    def kernel(rows_ref, weight_ref, out_ref):
        out_ref[...] = jnp.dot(rows_ref[...], weight_ref[...], preferred_element_type=jnp.float32)

    return pl.pallas_call(
        kernel,
        grid=(block_count,),
        in_specs=[
            pl.BlockSpec((row_count, depth), lambda n: (0, 0)),
            pl.BlockSpec((depth, width), lambda n: (0, first_block + n)),
        ],
        out_specs=pl.BlockSpec((row_count, width), lambda n: (0, n)),
        out_shape=jax.ShapeDtypeStruct((row_count, block_count * width), jnp.float32),
        cost_estimate=pl.CostEstimate(
            flops=2 * row_count * depth * block_count * width,
            transcendentals=0,
            bytes_accessed=2 * depth * (row_count + block_count * width)
            + 4 * row_count * block_count * width,
        ),
    )(rows, weight)


def layer_norm(values):
    center = values - jnp.mean(values, axis=-1, keepdims=True)
    spread = jnp.mean(center * center, axis=-1, keepdims=True)
    return center * lax.rsqrt(spread + EPS)


def head_norm(values, gain_row):
    power_mean = jnp.mean(values * values, axis=-1, keepdims=True)
    return (values * lax.rsqrt(power_mean + EPS) * gain_row).astype(jnp.bfloat16)


def rounded(values):
    narrow = lax.optimization_barrier(values.astype(jnp.bfloat16))
    return narrow.astype(jnp.float32)


def local(
    image_latent,
    control_latent,
    control_order,
    captions,
    caption_ids,
    modulation,
    qkv_weight,
    qk_gain,
    out_weight,
    zero_weight,
    proj_weight,
    final_mod,
    velocity_target,
):
    side_index = lax.axis_index("side")
    tp_index = lax.axis_index("tp")
    ctl_count = lax.axis_size("ctl")
    tp_count = lax.axis_size("tp")
    is_control = side_index == 0
    micro_count, img_rows, width_full = image_latent.shape
    text_rows = captions.shape[1]
    seq_rows = text_rows + img_rows
    local_heads = qkv_weight.shape[3]
    head_count = local_heads // HEAD_DIM
    half_width = width_full // tp_count
    quarter_width = half_width // 2
    flat_rows = micro_count * img_rows
    block_rows = width_full // (2 * ctl_count)
    aligned = jax.vmap(lambda latent, order_row: jnp.take(latent, order_row, axis=0))(
        control_latent, control_order
    )
    plain_rows = image_latent.astype(jnp.float32)
    hidden = plain_rows + jnp.where(is_control, 1.0, 0.0) * aligned.astype(jnp.float32)
    chosen = jnp.take(captions, caption_ids, axis=0).astype(jnp.float32)
    sequence = jnp.concatenate([chosen, hidden], axis=1)
    modulate = modulation[0]
    normed = (layer_norm(sequence) * (1.0 + modulate[:, 1:2]) + modulate[:, 0:1]).astype(
        jnp.bfloat16
    )
    text_flat = normed.reshape(micro_count * seq_rows, width_full)
    image_flat = normed[:, text_rows:].reshape(flat_rows, width_full)
    local_rows = qkv_weight.shape[1]
    own_cols = lax.dynamic_slice_in_dim(zero_weight, side_index * quarter_width, quarter_width, 1)
    packed = jnp.concatenate(
        [
            qkv_weight[0].reshape(local_rows, 3 * local_heads),
            out_weight[0].T,
            own_cols,
        ],
        axis=1,
    )
    gathered = ctl_gather(packed)
    count_rows = gathered.shape[0]
    out_cols = gathered[:, 3 * local_heads : 4 * local_heads]
    projected = block_matmul(text_flat, gathered, 0, 3, local_heads)
    projected = projected.reshape(micro_count, seq_rows, 3 * local_heads)
    query_acc = projected[:, text_rows:, :local_heads]
    pair_acc = projected[:, :, local_heads:]
    gain_pair = qk_gain[0]
    contract_last = (((1,), (1,)), ((), ()))
    other_out = lax.dynamic_slice_in_dim(out_cols, (1 - tp_index) * half_width, half_width, 0)
    own_out = lax.dynamic_slice_in_dim(out_cols, tp_index * half_width, half_width, 0)
    hid_half = lax.dynamic_slice_in_dim(hidden, tp_index * half_width, half_width, 2)
    gate_half = lax.dynamic_slice_in_dim(modulate[:, 2:3], tp_index * half_width, half_width, 2)
    act_halves = []
    act_rows = []
    for sample in range(micro_count):
        queries = head_norm(
            query_acc[sample].reshape(img_rows, head_count, HEAD_DIM), gain_pair[0]
        )
        pair_one = pair_acc[sample].reshape(seq_rows, 2, head_count, HEAD_DIM)
        keys_all = head_norm(pair_one[:, 0], gain_pair[1])
        values_all = pair_one[:, 1].astype(jnp.bfloat16)
        scores = jnp.einsum(
            "ihd,jhd->hij", queries, keys_all, preferred_element_type=jnp.float32
        ) / math.sqrt(HEAD_DIM)
        attend = jax.nn.softmax(scores, axis=-1).astype(jnp.bfloat16)
        mixed_heads = jnp.einsum(
            "hij,jhd->ihd", attend, values_all, preferred_element_type=jnp.float32
        )
        mixed_heads = mixed_heads.astype(jnp.bfloat16).reshape(img_rows, local_heads)
        other_part = lax.dot_general(
            mixed_heads, other_out, contract_last, preferred_element_type=jnp.float32
        ).astype(jnp.bfloat16)
        got_part = swap(other_part, "tp")
        own_part_heads = rounded(
            lax.dot_general(mixed_heads, own_out, contract_last, preferred_element_type=jnp.float32)
        )
        head_sum = own_part_heads + got_part.astype(jnp.float32)
        act_one = hid_half[sample] + gate_half[sample] * head_sum
        act_own = act_one.astype(jnp.bfloat16)
        act_got = lax.ppermute(act_own, ("side", "tp"), [(0, 1), (1, 0)])
        act_halves.append(act_one)
        act_rows.append(
            jnp.where(
                tp_index == 0,
                jnp.concatenate([act_own, act_got], axis=1),
                jnp.concatenate([act_got, act_own], axis=1),
            )
        )
    act_half = jnp.concatenate(act_halves, axis=0)
    act_narrow = jnp.concatenate(act_rows, axis=0)
    act_other = passed_along(act_narrow, "side", 1)
    control_rows = jnp.where(is_control, act_narrow, act_other)
    own_part = block_matmul(control_rows, gathered, 4, 1, local_heads)
    own_narrow = own_part.astype(jnp.bfloat16)
    other_narrow = partner(own_narrow, "side", 0)
    residual_narrow = jnp.where(
        is_control,
        jnp.concatenate([own_narrow, other_narrow], axis=1),
        jnp.concatenate([other_narrow, own_narrow], axis=1),
    )
    merged = act_half + residual_narrow.astype(jnp.float32)
    section_out = jnp.where(is_control, residual_narrow, merged.astype(jnp.bfloat16))
    final_half = lax.dynamic_slice_in_dim(final_mod, tp_index * half_width, half_width, 2)
    merged_rows = merged.reshape(micro_count, img_rows, half_width)
    row_total, squares = lax.psum(
        (
            jnp.sum(merged_rows, axis=-1, keepdims=True),
            jnp.sum(merged_rows * merged_rows, axis=-1, keepdims=True),
        ),
        "tp",
    )
    mean_val = row_total / width_full
    spread = squares / width_full - mean_val * mean_val
    scale_inv = lax.rsqrt(spread + EPS)
    unit_rows = (merged_rows - mean_val) * scale_inv
    final_in = (unit_rows * (1.0 + final_half[:, 1:2]) + final_half[:, 0:1]).astype(jnp.bfloat16)
    pred_part = jnp.dot(
        final_in.reshape(flat_rows, half_width), proj_weight, preferred_element_type=jnp.float32
    )
    prediction = pred_part + swap(pred_part, "tp")
    loss_factor = 4.0 / math.sqrt(micro_count * ctl_count * img_rows)
    grad_pred = (loss_factor * (prediction - velocity_target.reshape(flat_rows, -1))).astype(
        jnp.bfloat16
    )
    grad_unit = lax.dot_general(
        grad_pred, proj_weight, (((1,), (1,)), ((), ())), preferred_element_type=jnp.float32
    )
    grad_unit = grad_unit.reshape(micro_count, img_rows, half_width) * (1.0 + final_half[:, 1:2])
    first_sum, second_sum = lax.psum(
        (
            jnp.sum(grad_unit, axis=-1, keepdims=True),
            jnp.sum(grad_unit * unit_rows, axis=-1, keepdims=True),
        ),
        "tp",
    )
    grad_narrow = (
        (grad_unit - first_sum / width_full - unit_rows * (second_sum / width_full)) * scale_inv
    ).astype(jnp.bfloat16)
    grad_narrow = grad_narrow.reshape(flat_rows, half_width)
    returned = passed_along(grad_narrow, "side", -1)
    grad_rows_all = jnp.where(is_control, returned, grad_narrow)
    own_act = lax.dynamic_index_in_dim(
        control_rows.reshape(flat_rows, ctl_count, 2, block_rows), side_index, 2, keepdims=False
    )
    own_act = own_act.reshape(flat_rows, ctl_count * block_rows)
    product = lax.dot_general(
        own_act, grad_rows_all, (((0,), (0,)), ((), ())), preferred_element_type=jnp.float32
    )
    group_parts = rounded(product).astype(jnp.bfloat16).reshape(ctl_count, block_rows, half_width)
    received = lax.all_to_all(group_parts, "ctl", 0, 0, tiled=True)
    zero_grad = jnp.sum(received.astype(jnp.float32), axis=0)
    return (section_out.reshape(1, micro_count, img_rows, half_width), zero_grad)


def solution(mesh):
    return jax.shard_map(
        local,
        mesh=mesh,
        in_specs=(
            P("ctl", None, None),
            P("ctl", None, None),
            P("ctl", None),
            P("ctl", None, None),
            P("ctl"),
            P("side", "ctl", None, None),
            P("side", "ctl", None, "tp"),
            P("side", None, None),
            P("side", "tp", "ctl"),
            P("ctl", "tp"),
            P("tp", None),
            P("ctl", None, None),
            P("ctl", None, None),
        ),
        out_specs=(P("side", "ctl", None, "tp"), P(("ctl", "side"), "tp")),
        check_vma=False,
    )
```

```python
import math

import jax
import jax.numpy as jnp
from jax import lax
from jax.experimental import pallas as pl
from jax.sharding import PartitionSpec as P

HEAD_DIM = 128


EPS = 1e-06


def passed_along(shard, axis, by):
    length = lax.axis_size(axis)
    pairs = [(i, i + by) for i in range(length) if 0 <= i + by < length]
    return lax.ppermute(shard, axis, pairs)


def partner(value, axis, bit):
    mask = 2**bit
    pairs = [(source, source ^ mask) for source in range(lax.axis_size(axis))]
    return lax.ppermute(value, axis, pairs)


CTL_SHAPE = (4, 2, 4)


def ctl_coords(index):
    _, count_z, count_x = CTL_SHAPE
    return index // (count_z * count_x), (index // count_x) % count_z, index % count_x


def ctl_shift(value, step_y, flip_z, step_x):
    count_y, count_z, count_x = CTL_SHAPE
    pairs = []
    for source in range(count_y * count_z * count_x):
        at_y, at_z, at_x = ctl_coords(source)
        target = ((at_y + step_y) % count_y * count_z + (at_z ^ flip_z)) * count_x + (at_x + step_x) % count_x
        pairs.append((source, target))
    return lax.ppermute(value, "ctl", pairs)


def ring_stage(block, along_y, position):
    step = (1, 0) if along_y else (0, 1)
    forward = lambda value: ctl_shift(value, step[0], 0, step[1])
    backward = lambda value: ctl_shift(value, -step[0], 0, -step[1])
    from_before = forward(block)
    from_after = backward(block)
    half = block.shape[0] // 2
    far = jnp.concatenate([backward(from_after[:half]), forward(from_before[half:])], axis=0)
    relative = jnp.stack([block, from_after, far, from_before])
    return jnp.roll(relative, position, axis=0)


def ctl_gather(piece):
    at_y, at_z, at_x = ctl_coords(lax.axis_index("ctl"))
    rows, width = piece.shape
    paired = ctl_shift(piece, 0, 1, 0)
    pair = jnp.where(at_z == 0, jnp.stack([piece, paired]), jnp.stack([paired, piece]))
    split = width // 2
    first = ring_stage(pair[..., :split], False, at_x)
    first = ring_stage(jnp.swapaxes(first, 0, 1), True, at_y)
    second = ring_stage(pair[..., split:], True, at_y)
    second = ring_stage(second, False, at_x)
    second = jnp.moveaxis(second, 0, 2)
    return first.reshape(-1, split), second.reshape(-1, width - split)


def swap(value, axis):
    return lax.ppermute(value, axis, [(0, 1), (1, 0)])


def block_matmul(rows, weight, first_block, block_count, width):
    row_count, depth = rows.shape

    def kernel(rows_ref, weight_ref, out_ref):
        out_ref[...] = jnp.dot(rows_ref[...], weight_ref[...], preferred_element_type=jnp.float32)

    return pl.pallas_call(
        kernel,
        grid=(block_count,),
        in_specs=[
            pl.BlockSpec((row_count, depth), lambda n: (0, 0)),
            pl.BlockSpec((depth, width), lambda n: (0, first_block + n)),
        ],
        out_specs=pl.BlockSpec((row_count, width), lambda n: (0, n)),
        out_shape=jax.ShapeDtypeStruct((row_count, block_count * width), jnp.float32),
        cost_estimate=pl.CostEstimate(
            flops=2 * row_count * depth * block_count * width,
            transcendentals=0,
            bytes_accessed=2 * depth * (row_count + block_count * width)
            + 4 * row_count * block_count * width,
        ),
    )(rows, weight)


def layer_norm(values):
    center = values - jnp.mean(values, axis=-1, keepdims=True)
    spread = jnp.mean(center * center, axis=-1, keepdims=True)
    return center * lax.rsqrt(spread + EPS)


def head_norm(values, gain_row):
    power_mean = jnp.mean(values * values, axis=-1, keepdims=True)
    return (values * lax.rsqrt(power_mean + EPS) * gain_row).astype(jnp.bfloat16)


def rounded(values):
    narrow = lax.optimization_barrier(values.astype(jnp.bfloat16))
    return narrow.astype(jnp.float32)


def local(
    image_latent,
    control_latent,
    control_order,
    captions,
    caption_ids,
    modulation,
    qkv_weight,
    qk_gain,
    out_weight,
    zero_weight,
    proj_weight,
    final_mod,
    velocity_target,
):
    side_index = lax.axis_index("side")
    tp_index = lax.axis_index("tp")
    ctl_count = lax.axis_size("ctl")
    tp_count = lax.axis_size("tp")
    is_control = side_index == 0
    micro_count, img_rows, width_full = image_latent.shape
    text_rows = captions.shape[1]
    seq_rows = text_rows + img_rows
    local_heads = qkv_weight.shape[3]
    head_count = local_heads // HEAD_DIM
    half_width = width_full // tp_count
    quarter_width = half_width // 2
    flat_rows = micro_count * img_rows
    block_rows = width_full // (2 * ctl_count)
    aligned = jax.vmap(lambda latent, order_row: jnp.take(latent, order_row, axis=0))(
        control_latent, control_order
    )
    plain_rows = image_latent.astype(jnp.float32)
    hidden = plain_rows + jnp.where(is_control, 1.0, 0.0) * aligned.astype(jnp.float32)
    chosen = jnp.take(captions, caption_ids, axis=0).astype(jnp.float32)
    sequence = jnp.concatenate([chosen, hidden], axis=1)
    modulate = modulation[0]
    normed = (layer_norm(sequence) * (1.0 + modulate[:, 1:2]) + modulate[:, 0:1]).astype(
        jnp.bfloat16
    )
    text_flat = normed.reshape(micro_count * seq_rows, width_full)
    image_flat = normed[:, text_rows:].reshape(flat_rows, width_full)
    local_rows = qkv_weight.shape[1]
    own_cols = lax.dynamic_slice_in_dim(zero_weight, side_index * quarter_width, quarter_width, 1)
    packed = jnp.concatenate(
        [
            qkv_weight[0].reshape(local_rows, 3 * local_heads),
            out_weight[0].T,
            own_cols,
        ],
        axis=1,
    )
    front, back = ctl_gather(packed)
    count_rows = front.shape[0]
    narrow = local_heads // 2
    front_blocks = front.shape[1] // narrow
    out_cols = back[:, narrow : narrow + local_heads]
    projected = block_matmul(text_flat, front, 0, front_blocks, narrow)
    value_rest = block_matmul(text_flat, back, 0, 1, narrow)
    projected = projected.reshape(micro_count, seq_rows, front_blocks * narrow)
    query_acc = projected[:, text_rows:, :local_heads]
    key_acc = projected[:, :, local_heads : 2 * local_heads]
    value_acc = jnp.concatenate(
        [
            projected[:, :, 2 * local_heads :],
            value_rest.reshape(micro_count, seq_rows, narrow),
        ],
        axis=2,
    )
    gain_pair = qk_gain[0]
    contract_last = (((1,), (1,)), ((), ()))
    other_out = lax.dynamic_slice_in_dim(out_cols, (1 - tp_index) * half_width, half_width, 0)
    own_out = lax.dynamic_slice_in_dim(out_cols, tp_index * half_width, half_width, 0)
    hid_half = lax.dynamic_slice_in_dim(hidden, tp_index * half_width, half_width, 2)
    gate_half = lax.dynamic_slice_in_dim(modulate[:, 2:3], tp_index * half_width, half_width, 2)
    act_halves = []
    act_rows = []
    for sample in range(micro_count):
        queries = head_norm(
            query_acc[sample].reshape(img_rows, head_count, HEAD_DIM), gain_pair[0]
        )
        keys_all = head_norm(
            key_acc[sample].reshape(seq_rows, head_count, HEAD_DIM), gain_pair[1]
        )
        values_all = value_acc[sample].reshape(seq_rows, head_count, HEAD_DIM).astype(jnp.bfloat16)
        scores = jnp.einsum(
            "ihd,jhd->hij", queries, keys_all, preferred_element_type=jnp.float32
        ) / math.sqrt(HEAD_DIM)
        attend = jax.nn.softmax(scores, axis=-1).astype(jnp.bfloat16)
        mixed_heads = jnp.einsum(
            "hij,jhd->ihd", attend, values_all, preferred_element_type=jnp.float32
        )
        mixed_heads = mixed_heads.astype(jnp.bfloat16).reshape(img_rows, local_heads)
        other_part = lax.dot_general(
            mixed_heads, other_out, contract_last, preferred_element_type=jnp.float32
        ).astype(jnp.bfloat16)
        got_part = swap(other_part, "tp")
        own_part_heads = rounded(
            lax.dot_general(mixed_heads, own_out, contract_last, preferred_element_type=jnp.float32)
        )
        head_sum = own_part_heads + got_part.astype(jnp.float32)
        act_one = hid_half[sample] + gate_half[sample] * head_sum
        act_own = act_one.astype(jnp.bfloat16)
        act_got = lax.ppermute(act_own, ("side", "tp"), [(0, 1), (1, 0)])
        act_halves.append(act_one)
        act_rows.append(
            jnp.where(
                tp_index == 0,
                jnp.concatenate([act_own, act_got], axis=1),
                jnp.concatenate([act_got, act_own], axis=1),
            )
        )
    act_half = jnp.concatenate(act_halves, axis=0)
    act_narrow = jnp.concatenate(act_rows, axis=0)
    act_other = passed_along(act_narrow, "side", 1)
    control_rows = jnp.where(is_control, act_narrow, act_other)
    own_part = block_matmul(control_rows, back, 3, 2, narrow)
    own_narrow = own_part.astype(jnp.bfloat16)
    other_narrow = partner(own_narrow, "side", 0)
    residual_narrow = jnp.where(
        is_control,
        jnp.concatenate([own_narrow, other_narrow], axis=1),
        jnp.concatenate([other_narrow, own_narrow], axis=1),
    )
    merged = act_half + residual_narrow.astype(jnp.float32)
    section_out = jnp.where(is_control, residual_narrow, merged.astype(jnp.bfloat16))
    final_half = lax.dynamic_slice_in_dim(final_mod, tp_index * half_width, half_width, 2)
    merged_rows = merged.reshape(micro_count, img_rows, half_width)
    row_total, squares = lax.psum(
        (
            jnp.sum(merged_rows, axis=-1, keepdims=True),
            jnp.sum(merged_rows * merged_rows, axis=-1, keepdims=True),
        ),
        "tp",
    )
    mean_val = row_total / width_full
    spread = squares / width_full - mean_val * mean_val
    scale_inv = lax.rsqrt(spread + EPS)
    unit_rows = (merged_rows - mean_val) * scale_inv
    final_in = (unit_rows * (1.0 + final_half[:, 1:2]) + final_half[:, 0:1]).astype(jnp.bfloat16)
    pred_part = jnp.dot(
        final_in.reshape(flat_rows, half_width), proj_weight, preferred_element_type=jnp.float32
    )
    prediction = pred_part + swap(pred_part, "tp")
    loss_factor = 4.0 / math.sqrt(micro_count * ctl_count * img_rows)
    grad_pred = (loss_factor * (prediction - velocity_target.reshape(flat_rows, -1))).astype(
        jnp.bfloat16
    )
    grad_unit = lax.dot_general(
        grad_pred, proj_weight, (((1,), (1,)), ((), ())), preferred_element_type=jnp.float32
    )
    grad_unit = grad_unit.reshape(micro_count, img_rows, half_width) * (1.0 + final_half[:, 1:2])
    first_sum, second_sum = lax.psum(
        (
            jnp.sum(grad_unit, axis=-1, keepdims=True),
            jnp.sum(grad_unit * unit_rows, axis=-1, keepdims=True),
        ),
        "tp",
    )
    grad_narrow = (
        (grad_unit - first_sum / width_full - unit_rows * (second_sum / width_full)) * scale_inv
    ).astype(jnp.bfloat16)
    grad_narrow = grad_narrow.reshape(flat_rows, half_width)
    returned = passed_along(grad_narrow, "side", -1)
    grad_rows_all = jnp.where(is_control, returned, grad_narrow)
    own_act = lax.dynamic_index_in_dim(
        control_rows.reshape(flat_rows, ctl_count, 2, block_rows), side_index, 2, keepdims=False
    )
    own_act = own_act.reshape(flat_rows, ctl_count * block_rows)
    product = lax.dot_general(
        own_act, grad_rows_all, (((0,), (0,)), ((), ())), preferred_element_type=jnp.float32
    )
    group_parts = rounded(product).astype(jnp.bfloat16).reshape(ctl_count, block_rows, half_width)
    received = lax.all_to_all(group_parts, "ctl", 0, 0, tiled=True)
    zero_grad = jnp.sum(received.astype(jnp.float32), axis=0)
    return (section_out.reshape(1, micro_count, img_rows, half_width), zero_grad)


def solution(mesh):
    return jax.shard_map(
        local,
        mesh=mesh,
        in_specs=(
            P("ctl", None, None),
            P("ctl", None, None),
            P("ctl", None),
            P("ctl", None, None),
            P("ctl"),
            P("side", "ctl", None, None),
            P("side", "ctl", None, "tp"),
            P("side", None, None),
            P("side", "tp", "ctl"),
            P("ctl", "tp"),
            P("tp", None),
            P("ctl", None, None),
            P("ctl", None, None),
        ),
        out_specs=(P("side", "ctl", None, "tp"), P(("ctl", "side"), "tp")),
        check_vma=False,
    )
```

```python
import math

import jax
import jax.numpy as jnp
from jax import lax
from jax.experimental import pallas as pl
from jax.sharding import PartitionSpec as P

HEAD_DIM = 128


EPS = 1e-06


def passed_along(shard, axis, by):
    length = lax.axis_size(axis)
    pairs = [(i, i + by) for i in range(length) if 0 <= i + by < length]
    return lax.ppermute(shard, axis, pairs)


def partner(value, axis, bit):
    mask = 2**bit
    pairs = [(source, source ^ mask) for source in range(lax.axis_size(axis))]
    return lax.ppermute(value, axis, pairs)


CTL_SHAPE = (4, 2, 4)


def ctl_coords(index):
    _, count_z, count_x = CTL_SHAPE
    return index // (count_z * count_x), (index // count_x) % count_z, index % count_x


def ctl_shift(value, step_y, flip_z, step_x):
    count_y, count_z, count_x = CTL_SHAPE
    pairs = []
    for source in range(count_y * count_z * count_x):
        at_y, at_z, at_x = ctl_coords(source)
        target = ((at_y + step_y) % count_y * count_z + (at_z ^ flip_z)) * count_x + (at_x + step_x) % count_x
        pairs.append((source, target))
    return lax.ppermute(value, "ctl", pairs)


def ring_stage(block, along_y, position):
    step = (1, 0) if along_y else (0, 1)
    forward = lambda value: ctl_shift(value, step[0], 0, step[1])
    backward = lambda value: ctl_shift(value, -step[0], 0, -step[1])
    from_before = forward(block)
    from_after = backward(block)
    half = block.shape[0] // 2
    far = jnp.concatenate([backward(from_after[:half]), forward(from_before[half:])], axis=0)
    relative = jnp.stack([block, from_after, far, from_before])
    if position is None:
        return relative
    return jnp.roll(relative, position, axis=0)


def ctl_gather(piece):
    at_y, at_z, at_x = ctl_coords(lax.axis_index("ctl"))
    rows, width = piece.shape
    paired = ctl_shift(piece, 0, 1, 0)
    pair = jnp.where(at_z == 0, jnp.stack([piece, paired]), jnp.stack([paired, piece]))
    split = width // 2
    first = ring_stage(pair[..., :split], False, at_x)
    first = ring_stage(jnp.swapaxes(first, 0, 1), True, at_y)
    second = ring_stage(pair[..., split:], True, at_y)
    second = ring_stage(second, False, None)
    return first.reshape(-1, split), second.reshape(-1, width - split)


def x_relative(rows):
    count_y, count_z, count_x = CTL_SHAPE
    at_x = ctl_coords(lax.axis_index("ctl"))[2]
    blocks = rows.reshape(rows.shape[0], count_y, count_z, count_x, -1)
    blocks = jnp.roll(blocks, -at_x, axis=3)
    return jnp.moveaxis(blocks, 3, 1).reshape(rows.shape)


def x_absolute(weight):
    count_y, count_z, count_x = CTL_SHAPE
    at_x = ctl_coords(lax.axis_index("ctl"))[2]
    blocks = weight.reshape(count_x, count_y, count_z, -1, weight.shape[1])
    blocks = jnp.roll(blocks, at_x, axis=0)
    return jnp.moveaxis(blocks, 0, 2).reshape(weight.shape)


def swap(value, axis):
    return lax.ppermute(value, axis, [(0, 1), (1, 0)])


def block_matmul(rows, weight, first_block, block_count, width):
    row_count, depth = rows.shape

    def kernel(rows_ref, weight_ref, out_ref):
        out_ref[...] = jnp.dot(rows_ref[...], weight_ref[...], preferred_element_type=jnp.float32)

    return pl.pallas_call(
        kernel,
        grid=(block_count,),
        in_specs=[
            pl.BlockSpec((row_count, depth), lambda n: (0, 0)),
            pl.BlockSpec((depth, width), lambda n: (0, first_block + n)),
        ],
        out_specs=pl.BlockSpec((row_count, width), lambda n: (0, n)),
        out_shape=jax.ShapeDtypeStruct((row_count, block_count * width), jnp.float32),
        cost_estimate=pl.CostEstimate(
            flops=2 * row_count * depth * block_count * width,
            transcendentals=0,
            bytes_accessed=2 * depth * (row_count + block_count * width)
            + 4 * row_count * block_count * width,
        ),
    )(rows, weight)


def layer_norm(values):
    center = values - jnp.mean(values, axis=-1, keepdims=True)
    spread = jnp.mean(center * center, axis=-1, keepdims=True)
    return center * lax.rsqrt(spread + EPS)


def head_norm(values, gain_row):
    power_mean = jnp.mean(values * values, axis=-1, keepdims=True)
    return (values * lax.rsqrt(power_mean + EPS) * gain_row).astype(jnp.bfloat16)


def rounded(values):
    narrow = lax.optimization_barrier(values.astype(jnp.bfloat16))
    return narrow.astype(jnp.float32)


def local(
    image_latent,
    control_latent,
    control_order,
    captions,
    caption_ids,
    modulation,
    qkv_weight,
    qk_gain,
    out_weight,
    zero_weight,
    proj_weight,
    final_mod,
    velocity_target,
):
    side_index = lax.axis_index("side")
    tp_index = lax.axis_index("tp")
    ctl_count = lax.axis_size("ctl")
    tp_count = lax.axis_size("tp")
    is_control = side_index == 0
    micro_count, img_rows, width_full = image_latent.shape
    text_rows = captions.shape[1]
    seq_rows = text_rows + img_rows
    local_heads = qkv_weight.shape[3]
    head_count = local_heads // HEAD_DIM
    half_width = width_full // tp_count
    quarter_width = half_width // 2
    flat_rows = micro_count * img_rows
    block_rows = width_full // (2 * ctl_count)
    aligned = jax.vmap(lambda latent, order_row: jnp.take(latent, order_row, axis=0))(
        control_latent, control_order
    )
    plain_rows = image_latent.astype(jnp.float32)
    hidden = plain_rows + jnp.where(is_control, 1.0, 0.0) * aligned.astype(jnp.float32)
    chosen = jnp.take(captions, caption_ids, axis=0).astype(jnp.float32)
    sequence = jnp.concatenate([chosen, hidden], axis=1)
    modulate = modulation[0]
    normed = (layer_norm(sequence) * (1.0 + modulate[:, 1:2]) + modulate[:, 0:1]).astype(
        jnp.bfloat16
    )
    text_flat = normed.reshape(micro_count * seq_rows, width_full)
    image_flat = normed[:, text_rows:].reshape(flat_rows, width_full)
    local_rows = qkv_weight.shape[1]
    own_cols = lax.dynamic_slice_in_dim(zero_weight, side_index * quarter_width, quarter_width, 1)
    packed = jnp.concatenate(
        [
            qkv_weight[0].reshape(local_rows, 3 * local_heads),
            out_weight[0].T,
            own_cols,
        ],
        axis=1,
    )
    front, back = ctl_gather(packed)
    count_rows = front.shape[0]
    narrow = local_heads // 2
    front_blocks = front.shape[1] // narrow
    out_cols = x_absolute(back[:, narrow : narrow + local_heads])
    projected = block_matmul(text_flat, front, 0, front_blocks, narrow)
    value_rest = block_matmul(x_relative(text_flat), back, 0, 1, narrow)
    projected = projected.reshape(micro_count, seq_rows, front_blocks * narrow)
    query_acc = projected[:, text_rows:, :local_heads]
    key_acc = projected[:, :, local_heads : 2 * local_heads]
    value_acc = jnp.concatenate(
        [
            projected[:, :, 2 * local_heads :],
            value_rest.reshape(micro_count, seq_rows, narrow),
        ],
        axis=2,
    )
    gain_pair = qk_gain[0]
    contract_last = (((1,), (1,)), ((), ()))
    other_out = lax.dynamic_slice_in_dim(out_cols, (1 - tp_index) * half_width, half_width, 0)
    own_out = lax.dynamic_slice_in_dim(out_cols, tp_index * half_width, half_width, 0)
    hid_half = lax.dynamic_slice_in_dim(hidden, tp_index * half_width, half_width, 2)
    gate_half = lax.dynamic_slice_in_dim(modulate[:, 2:3], tp_index * half_width, half_width, 2)
    act_halves = []
    act_rows = []
    for sample in range(micro_count):
        queries = head_norm(
            query_acc[sample].reshape(img_rows, head_count, HEAD_DIM), gain_pair[0]
        )
        keys_all = head_norm(
            key_acc[sample].reshape(seq_rows, head_count, HEAD_DIM), gain_pair[1]
        )
        values_all = value_acc[sample].reshape(seq_rows, head_count, HEAD_DIM).astype(jnp.bfloat16)
        scores = jnp.einsum(
            "ihd,jhd->hij", queries, keys_all, preferred_element_type=jnp.float32
        ) / math.sqrt(HEAD_DIM)
        attend = jax.nn.softmax(scores, axis=-1).astype(jnp.bfloat16)
        mixed_heads = jnp.einsum(
            "hij,jhd->ihd", attend, values_all, preferred_element_type=jnp.float32
        )
        mixed_heads = mixed_heads.astype(jnp.bfloat16).reshape(img_rows, local_heads)
        other_part = lax.dot_general(
            mixed_heads, other_out, contract_last, preferred_element_type=jnp.float32
        ).astype(jnp.bfloat16)
        got_part = swap(other_part, "tp")
        own_part_heads = rounded(
            lax.dot_general(mixed_heads, own_out, contract_last, preferred_element_type=jnp.float32)
        )
        head_sum = own_part_heads + got_part.astype(jnp.float32)
        act_one = hid_half[sample] + gate_half[sample] * head_sum
        act_own = act_one.astype(jnp.bfloat16)
        act_got = lax.ppermute(act_own, ("side", "tp"), [(0, 1), (1, 0)])
        act_halves.append(act_one)
        act_rows.append(
            jnp.where(
                tp_index == 0,
                jnp.concatenate([act_own, act_got], axis=1),
                jnp.concatenate([act_got, act_own], axis=1),
            )
        )
    act_half = jnp.concatenate(act_halves, axis=0)
    act_narrow = jnp.concatenate(act_rows, axis=0)
    act_other = passed_along(act_narrow, "side", 1)
    control_rows = jnp.where(is_control, act_narrow, act_other)
    own_part = block_matmul(x_relative(control_rows), back, 3, 2, narrow)
    own_narrow = own_part.astype(jnp.bfloat16)
    other_narrow = partner(own_narrow, "side", 0)
    residual_narrow = jnp.where(
        is_control,
        jnp.concatenate([own_narrow, other_narrow], axis=1),
        jnp.concatenate([other_narrow, own_narrow], axis=1),
    )
    merged = act_half + residual_narrow.astype(jnp.float32)
    section_out = jnp.where(is_control, residual_narrow, merged.astype(jnp.bfloat16))
    final_half = lax.dynamic_slice_in_dim(final_mod, tp_index * half_width, half_width, 2)
    merged_rows = merged.reshape(micro_count, img_rows, half_width)
    row_total, squares = lax.psum(
        (
            jnp.sum(merged_rows, axis=-1, keepdims=True),
            jnp.sum(merged_rows * merged_rows, axis=-1, keepdims=True),
        ),
        "tp",
    )
    mean_val = row_total / width_full
    spread = squares / width_full - mean_val * mean_val
    scale_inv = lax.rsqrt(spread + EPS)
    unit_rows = (merged_rows - mean_val) * scale_inv
    final_in = (unit_rows * (1.0 + final_half[:, 1:2]) + final_half[:, 0:1]).astype(jnp.bfloat16)
    pred_part = jnp.dot(
        final_in.reshape(flat_rows, half_width), proj_weight, preferred_element_type=jnp.float32
    )
    prediction = pred_part + swap(pred_part, "tp")
    loss_factor = 4.0 / math.sqrt(micro_count * ctl_count * img_rows)
    grad_pred = (loss_factor * (prediction - velocity_target.reshape(flat_rows, -1))).astype(
        jnp.bfloat16
    )
    grad_unit = lax.dot_general(
        grad_pred, proj_weight, (((1,), (1,)), ((), ())), preferred_element_type=jnp.float32
    )
    grad_unit = grad_unit.reshape(micro_count, img_rows, half_width) * (1.0 + final_half[:, 1:2])
    first_sum, second_sum = lax.psum(
        (
            jnp.sum(grad_unit, axis=-1, keepdims=True),
            jnp.sum(grad_unit * unit_rows, axis=-1, keepdims=True),
        ),
        "tp",
    )
    grad_narrow = (
        (grad_unit - first_sum / width_full - unit_rows * (second_sum / width_full)) * scale_inv
    ).astype(jnp.bfloat16)
    grad_narrow = grad_narrow.reshape(flat_rows, half_width)
    returned = passed_along(grad_narrow, "side", -1)
    grad_rows_all = jnp.where(is_control, returned, grad_narrow)
    own_act = lax.dynamic_index_in_dim(
        control_rows.reshape(flat_rows, ctl_count, 2, block_rows), side_index, 2, keepdims=False
    )
    own_act = own_act.reshape(flat_rows, ctl_count * block_rows)
    product = lax.dot_general(
        own_act, grad_rows_all, (((0,), (0,)), ((), ())), preferred_element_type=jnp.float32
    )
    group_parts = rounded(product).astype(jnp.bfloat16).reshape(ctl_count, block_rows, half_width)
    received = lax.all_to_all(group_parts, "ctl", 0, 0, tiled=True)
    zero_grad = jnp.sum(received.astype(jnp.float32), axis=0)
    return (section_out.reshape(1, micro_count, img_rows, half_width), zero_grad)


def solution(mesh):
    return jax.shard_map(
        local,
        mesh=mesh,
        in_specs=(
            P("ctl", None, None),
            P("ctl", None, None),
            P("ctl", None),
            P("ctl", None, None),
            P("ctl"),
            P("side", "ctl", None, None),
            P("side", "ctl", None, "tp"),
            P("side", None, None),
            P("side", "tp", "ctl"),
            P("ctl", "tp"),
            P("tp", None),
            P("ctl", None, None),
            P("ctl", None, None),
        ),
        out_specs=(P("side", "ctl", None, "tp"), P(("ctl", "side"), "tp")),
        check_vma=False,
    )
```

```python
import math

import jax
import jax.numpy as jnp
from jax import lax
from jax.experimental import pallas as pl
from jax.sharding import PartitionSpec as P

HEAD_DIM = 128


EPS = 1e-06


def passed_along(shard, axis, by):
    length = lax.axis_size(axis)
    pairs = [(i, i + by) for i in range(length) if 0 <= i + by < length]
    return lax.ppermute(shard, axis, pairs)


def partner(value, axis, bit):
    mask = 2**bit
    pairs = [(source, source ^ mask) for source in range(lax.axis_size(axis))]
    return lax.ppermute(value, axis, pairs)


CTL_SHAPE = (4, 2, 4)


def ctl_coords(index):
    _, count_z, count_x = CTL_SHAPE
    return index // (count_z * count_x), (index // count_x) % count_z, index % count_x


def ctl_shift(value, step_y, flip_z, step_x):
    count_y, count_z, count_x = CTL_SHAPE
    pairs = []
    for source in range(count_y * count_z * count_x):
        at_y, at_z, at_x = ctl_coords(source)
        target = ((at_y + step_y) % count_y * count_z + (at_z ^ flip_z)) * count_x + (at_x + step_x) % count_x
        pairs.append((source, target))
    return lax.ppermute(value, "ctl", pairs)


def ring_stage(block, along_y, position):
    step = (1, 0) if along_y else (0, 1)
    forward = lambda value: ctl_shift(value, step[0], 0, step[1])
    backward = lambda value: ctl_shift(value, -step[0], 0, -step[1])
    from_before = forward(block)
    from_after = backward(block)
    half = block.shape[0] // 2
    far = jnp.concatenate([backward(from_after[:half]), forward(from_before[half:])], axis=0)
    relative = jnp.stack([block, from_after, far, from_before])
    return jnp.roll(relative, position, axis=0)


def ctl_gather(piece, split):
    at_y, at_z, at_x = ctl_coords(lax.axis_index("ctl"))
    rows, width = piece.shape
    paired = ctl_shift(piece, 0, 1, 0)
    pair = jnp.where(at_z == 0, jnp.stack([piece, paired]), jnp.stack([paired, piece]))
    first = ring_stage(pair[..., :split], False, at_x)
    first = ring_stage(jnp.swapaxes(first, 0, 1), True, at_y)
    second = ring_stage(pair[..., split:], True, at_y)
    second = ring_stage(second, False, at_x)
    second = jnp.moveaxis(second, 0, 2)
    return first.reshape(-1, split), second.reshape(-1, width - split)


def swap(value, axis):
    return lax.ppermute(value, axis, [(0, 1), (1, 0)])


def block_matmul(rows, weight, first_block, block_count, width):
    row_count, depth = rows.shape

    def kernel(rows_ref, weight_ref, out_ref):
        out_ref[...] = jnp.dot(rows_ref[...], weight_ref[...], preferred_element_type=jnp.float32)

    return pl.pallas_call(
        kernel,
        grid=(block_count,),
        in_specs=[
            pl.BlockSpec((row_count, depth), lambda n: (0, 0)),
            pl.BlockSpec((depth, width), lambda n: (0, first_block + n)),
        ],
        out_specs=pl.BlockSpec((row_count, width), lambda n: (0, n)),
        out_shape=jax.ShapeDtypeStruct((row_count, block_count * width), jnp.float32),
        cost_estimate=pl.CostEstimate(
            flops=2 * row_count * depth * block_count * width,
            transcendentals=0,
            bytes_accessed=2 * depth * (row_count + block_count * width)
            + 4 * row_count * block_count * width,
        ),
    )(rows, weight)


def layer_norm(values):
    center = values - jnp.mean(values, axis=-1, keepdims=True)
    spread = jnp.mean(center * center, axis=-1, keepdims=True)
    return center * lax.rsqrt(spread + EPS)


def head_norm(values, gain_row):
    power_mean = jnp.mean(values * values, axis=-1, keepdims=True)
    return (values * lax.rsqrt(power_mean + EPS) * gain_row).astype(jnp.bfloat16)


def rounded(values):
    narrow = lax.optimization_barrier(values.astype(jnp.bfloat16))
    return narrow.astype(jnp.float32)


def local(
    image_latent,
    control_latent,
    control_order,
    captions,
    caption_ids,
    modulation,
    qkv_weight,
    qk_gain,
    out_weight,
    zero_weight,
    proj_weight,
    final_mod,
    velocity_target,
):
    side_index = lax.axis_index("side")
    tp_index = lax.axis_index("tp")
    ctl_count = lax.axis_size("ctl")
    tp_count = lax.axis_size("tp")
    is_control = side_index == 0
    micro_count, img_rows, width_full = image_latent.shape
    text_rows = captions.shape[1]
    seq_rows = text_rows + img_rows
    local_heads = qkv_weight.shape[3]
    head_count = local_heads // HEAD_DIM
    half_width = width_full // tp_count
    quarter_width = half_width // 2
    flat_rows = micro_count * img_rows
    block_rows = width_full // (2 * ctl_count)
    aligned = jax.vmap(lambda latent, order_row: jnp.take(latent, order_row, axis=0))(
        control_latent, control_order
    )
    plain_rows = image_latent.astype(jnp.float32)
    hidden = plain_rows + jnp.where(is_control, 1.0, 0.0) * aligned.astype(jnp.float32)
    chosen = jnp.take(captions, caption_ids, axis=0).astype(jnp.float32)
    sequence = jnp.concatenate([chosen, hidden], axis=1)
    modulate = modulation[0]
    normed = (layer_norm(sequence) * (1.0 + modulate[:, 1:2]) + modulate[:, 0:1]).astype(
        jnp.bfloat16
    )
    text_flat = normed.reshape(micro_count * seq_rows, width_full)
    image_flat = normed[:, text_rows:].reshape(flat_rows, width_full)
    local_rows = qkv_weight.shape[1]
    own_cols = lax.dynamic_slice_in_dim(zero_weight, side_index * quarter_width, quarter_width, 1)
    packed = jnp.concatenate(
        [
            qkv_weight[0].reshape(local_rows, 3 * local_heads),
            out_weight[0].T,
            own_cols,
        ],
        axis=1,
    )
    front, back = ctl_gather(packed, 3 * local_heads)
    count_rows = front.shape[0]
    out_cols = back[:, :local_heads]
    projected = block_matmul(text_flat, front, 0, 3, local_heads)
    projected = projected.reshape(micro_count, seq_rows, 3 * local_heads)
    query_acc = projected[:, text_rows:, :local_heads]
    key_acc = projected[:, :, local_heads : 2 * local_heads]
    value_acc = projected[:, :, 2 * local_heads :]
    gain_pair = qk_gain[0]
    contract_last = (((1,), (1,)), ((), ()))
    other_out = lax.dynamic_slice_in_dim(out_cols, (1 - tp_index) * half_width, half_width, 0)
    own_out = lax.dynamic_slice_in_dim(out_cols, tp_index * half_width, half_width, 0)
    hid_half = lax.dynamic_slice_in_dim(hidden, tp_index * half_width, half_width, 2)
    gate_half = lax.dynamic_slice_in_dim(modulate[:, 2:3], tp_index * half_width, half_width, 2)
    act_halves = []
    act_rows = []
    for sample in range(micro_count):
        queries = head_norm(
            query_acc[sample].reshape(img_rows, head_count, HEAD_DIM), gain_pair[0]
        )
        keys_all = head_norm(
            key_acc[sample].reshape(seq_rows, head_count, HEAD_DIM), gain_pair[1]
        )
        values_all = value_acc[sample].reshape(seq_rows, head_count, HEAD_DIM).astype(jnp.bfloat16)
        scores = jnp.einsum(
            "ihd,jhd->hij", queries, keys_all, preferred_element_type=jnp.float32
        ) / math.sqrt(HEAD_DIM)
        attend = jax.nn.softmax(scores, axis=-1).astype(jnp.bfloat16)
        mixed_heads = jnp.einsum(
            "hij,jhd->ihd", attend, values_all, preferred_element_type=jnp.float32
        )
        mixed_heads = mixed_heads.astype(jnp.bfloat16).reshape(img_rows, local_heads)
        other_part = lax.dot_general(
            mixed_heads, other_out, contract_last, preferred_element_type=jnp.float32
        ).astype(jnp.bfloat16)
        got_part = swap(other_part, "tp")
        own_part_heads = rounded(
            lax.dot_general(mixed_heads, own_out, contract_last, preferred_element_type=jnp.float32)
        )
        head_sum = own_part_heads + got_part.astype(jnp.float32)
        act_one = hid_half[sample] + gate_half[sample] * head_sum
        act_own = act_one.astype(jnp.bfloat16)
        act_got = lax.ppermute(act_own, ("side", "tp"), [(0, 1), (1, 0)])
        act_halves.append(act_one)
        act_rows.append(
            jnp.where(
                tp_index == 0,
                jnp.concatenate([act_own, act_got], axis=1),
                jnp.concatenate([act_got, act_own], axis=1),
            )
        )
    act_half = jnp.concatenate(act_halves, axis=0)
    act_narrow = jnp.concatenate(act_rows, axis=0)
    act_other = passed_along(act_narrow, "side", 1)
    control_rows = jnp.where(is_control, act_narrow, act_other)
    own_part = block_matmul(control_rows, back, 1, 1, local_heads)
    own_narrow = own_part.astype(jnp.bfloat16)
    other_narrow = partner(own_narrow, "side", 0)
    residual_narrow = jnp.where(
        is_control,
        jnp.concatenate([own_narrow, other_narrow], axis=1),
        jnp.concatenate([other_narrow, own_narrow], axis=1),
    )
    merged = act_half + residual_narrow.astype(jnp.float32)
    section_out = jnp.where(is_control, residual_narrow, merged.astype(jnp.bfloat16))
    final_half = lax.dynamic_slice_in_dim(final_mod, tp_index * half_width, half_width, 2)
    merged_rows = merged.reshape(micro_count, img_rows, half_width)
    row_total, squares = lax.psum(
        (
            jnp.sum(merged_rows, axis=-1, keepdims=True),
            jnp.sum(merged_rows * merged_rows, axis=-1, keepdims=True),
        ),
        "tp",
    )
    mean_val = row_total / width_full
    spread = squares / width_full - mean_val * mean_val
    scale_inv = lax.rsqrt(spread + EPS)
    unit_rows = (merged_rows - mean_val) * scale_inv
    final_in = (unit_rows * (1.0 + final_half[:, 1:2]) + final_half[:, 0:1]).astype(jnp.bfloat16)
    pred_part = jnp.dot(
        final_in.reshape(flat_rows, half_width), proj_weight, preferred_element_type=jnp.float32
    )
    prediction = pred_part + swap(pred_part, "tp")
    loss_factor = 4.0 / math.sqrt(micro_count * ctl_count * img_rows)
    grad_pred = (loss_factor * (prediction - velocity_target.reshape(flat_rows, -1))).astype(
        jnp.bfloat16
    )
    grad_unit = lax.dot_general(
        grad_pred, proj_weight, (((1,), (1,)), ((), ())), preferred_element_type=jnp.float32
    )
    grad_unit = grad_unit.reshape(micro_count, img_rows, half_width) * (1.0 + final_half[:, 1:2])
    first_sum, second_sum = lax.psum(
        (
            jnp.sum(grad_unit, axis=-1, keepdims=True),
            jnp.sum(grad_unit * unit_rows, axis=-1, keepdims=True),
        ),
        "tp",
    )
    grad_narrow = (
        (grad_unit - first_sum / width_full - unit_rows * (second_sum / width_full)) * scale_inv
    ).astype(jnp.bfloat16)
    grad_narrow = grad_narrow.reshape(flat_rows, half_width)
    returned = passed_along(grad_narrow, "side", -1)
    grad_rows_all = jnp.where(is_control, returned, grad_narrow)
    own_act = lax.dynamic_index_in_dim(
        control_rows.reshape(flat_rows, ctl_count, 2, block_rows), side_index, 2, keepdims=False
    )
    own_act = own_act.reshape(flat_rows, ctl_count * block_rows)
    product = lax.dot_general(
        own_act, grad_rows_all, (((0,), (0,)), ((), ())), preferred_element_type=jnp.float32
    )
    group_parts = rounded(product).astype(jnp.bfloat16).reshape(ctl_count, block_rows, half_width)
    received = lax.all_to_all(group_parts, "ctl", 0, 0, tiled=True)
    zero_grad = jnp.sum(received.astype(jnp.float32), axis=0)
    return (section_out.reshape(1, micro_count, img_rows, half_width), zero_grad)


def solution(mesh):
    return jax.shard_map(
        local,
        mesh=mesh,
        in_specs=(
            P("ctl", None, None),
            P("ctl", None, None),
            P("ctl", None),
            P("ctl", None, None),
            P("ctl"),
            P("side", "ctl", None, None),
            P("side", "ctl", None, "tp"),
            P("side", None, None),
            P("side", "tp", "ctl"),
            P("ctl", "tp"),
            P("tp", None),
            P("ctl", None, None),
            P("ctl", None, None),
        ),
        out_specs=(P("side", "ctl", None, "tp"), P(("ctl", "side"), "tp")),
        check_vma=False,
    )
```

```python
import math

import jax
import jax.numpy as jnp
from jax import lax
from jax.experimental import pallas as pl
from jax.sharding import PartitionSpec as P

HEAD_DIM = 128


EPS = 1e-06


def passed_along(shard, axis, by):
    length = lax.axis_size(axis)
    pairs = [(i, i + by) for i in range(length) if 0 <= i + by < length]
    return lax.ppermute(shard, axis, pairs)


def partner(value, axis, bit):
    mask = 2**bit
    pairs = [(source, source ^ mask) for source in range(lax.axis_size(axis))]
    return lax.ppermute(value, axis, pairs)


CTL_SHAPE = (4, 2, 4)


def ctl_coords(index):
    _, count_z, count_x = CTL_SHAPE
    return index // (count_z * count_x), (index // count_x) % count_z, index % count_x


def ctl_shift(value, step_y, flip_z, step_x):
    count_y, count_z, count_x = CTL_SHAPE
    pairs = []
    for source in range(count_y * count_z * count_x):
        at_y, at_z, at_x = ctl_coords(source)
        target = ((at_y + step_y) % count_y * count_z + (at_z ^ flip_z)) * count_x + (at_x + step_x) % count_x
        pairs.append((source, target))
    return lax.ppermute(value, "ctl", pairs)


def ring_stage(block, along_y, position):
    step = (1, 0) if along_y else (0, 1)
    forward = lambda value: ctl_shift(value, step[0], 0, step[1])
    backward = lambda value: ctl_shift(value, -step[0], 0, -step[1])
    from_before = forward(block)
    from_after = backward(block)
    half = block.shape[0] // 2
    far = jnp.concatenate([backward(from_after[:half]), forward(from_before[half:])], axis=0)
    relative = jnp.stack([block, from_after, far, from_before])
    return jnp.roll(relative, position, axis=0)


def ctl_gather(piece):
    at_y, at_z, at_x = ctl_coords(lax.axis_index("ctl"))
    split = piece.shape[1] // 2

    def both_rings(block):
        first = ring_stage(block[:, :split], False, at_x)
        first = ring_stage(first, True, at_y)
        second = ring_stage(block[:, split:], True, at_y)
        second = jnp.swapaxes(ring_stage(second, False, at_x), 0, 1)
        return first, second

    own_first, own_second = both_rings(piece)
    paired_first, paired_second = both_rings(ctl_shift(piece, 0, 1, 0))

    def join(own, paired):
        low = jnp.where(at_z == 0, own, paired)
        high = jnp.where(at_z == 0, paired, own)
        return jnp.stack([low, high], axis=1).reshape(-1, own.shape[-1])

    return join(own_first, paired_first), join(own_second, paired_second)


def swap(value, axis):
    return lax.ppermute(value, axis, [(0, 1), (1, 0)])


def block_matmul(rows, weight, first_block, block_count, width):
    row_count, depth = rows.shape

    def kernel(rows_ref, weight_ref, out_ref):
        out_ref[...] = jnp.dot(rows_ref[...], weight_ref[...], preferred_element_type=jnp.float32)

    return pl.pallas_call(
        kernel,
        grid=(block_count,),
        in_specs=[
            pl.BlockSpec((row_count, depth), lambda n: (0, 0)),
            pl.BlockSpec((depth, width), lambda n: (0, first_block + n)),
        ],
        out_specs=pl.BlockSpec((row_count, width), lambda n: (0, n)),
        out_shape=jax.ShapeDtypeStruct((row_count, block_count * width), jnp.float32),
        cost_estimate=pl.CostEstimate(
            flops=2 * row_count * depth * block_count * width,
            transcendentals=0,
            bytes_accessed=2 * depth * (row_count + block_count * width)
            + 4 * row_count * block_count * width,
        ),
    )(rows, weight)


def layer_norm(values):
    center = values - jnp.mean(values, axis=-1, keepdims=True)
    spread = jnp.mean(center * center, axis=-1, keepdims=True)
    return center * lax.rsqrt(spread + EPS)


def head_norm(values, gain_row):
    power_mean = jnp.mean(values * values, axis=-1, keepdims=True)
    return (values * lax.rsqrt(power_mean + EPS) * gain_row).astype(jnp.bfloat16)


def rounded(values):
    narrow = lax.optimization_barrier(values.astype(jnp.bfloat16))
    return narrow.astype(jnp.float32)


def local(
    image_latent,
    control_latent,
    control_order,
    captions,
    caption_ids,
    modulation,
    qkv_weight,
    qk_gain,
    out_weight,
    zero_weight,
    proj_weight,
    final_mod,
    velocity_target,
):
    side_index = lax.axis_index("side")
    tp_index = lax.axis_index("tp")
    ctl_count = lax.axis_size("ctl")
    tp_count = lax.axis_size("tp")
    is_control = side_index == 0
    micro_count, img_rows, width_full = image_latent.shape
    text_rows = captions.shape[1]
    seq_rows = text_rows + img_rows
    local_heads = qkv_weight.shape[3]
    head_count = local_heads // HEAD_DIM
    half_width = width_full // tp_count
    quarter_width = half_width // 2
    flat_rows = micro_count * img_rows
    block_rows = width_full // (2 * ctl_count)
    aligned = jax.vmap(lambda latent, order_row: jnp.take(latent, order_row, axis=0))(
        control_latent, control_order
    )
    plain_rows = image_latent.astype(jnp.float32)
    hidden = plain_rows + jnp.where(is_control, 1.0, 0.0) * aligned.astype(jnp.float32)
    chosen = jnp.take(captions, caption_ids, axis=0).astype(jnp.float32)
    sequence = jnp.concatenate([chosen, hidden], axis=1)
    modulate = modulation[0]
    normed = (layer_norm(sequence) * (1.0 + modulate[:, 1:2]) + modulate[:, 0:1]).astype(
        jnp.bfloat16
    )
    text_flat = normed.reshape(micro_count * seq_rows, width_full)
    image_flat = normed[:, text_rows:].reshape(flat_rows, width_full)
    local_rows = qkv_weight.shape[1]
    own_cols = lax.dynamic_slice_in_dim(zero_weight, side_index * quarter_width, quarter_width, 1)
    packed = jnp.concatenate(
        [
            qkv_weight[0].reshape(local_rows, 3 * local_heads),
            out_weight[0].T,
            own_cols,
        ],
        axis=1,
    )
    front, back = ctl_gather(packed)
    count_rows = front.shape[0]
    narrow = local_heads // 2
    front_blocks = front.shape[1] // narrow
    out_cols = back[:, narrow : narrow + local_heads]
    projected = block_matmul(text_flat, front, 0, front_blocks, narrow)
    value_rest = block_matmul(text_flat, back, 0, 1, narrow)
    projected = projected.reshape(micro_count, seq_rows, front_blocks * narrow)
    query_acc = projected[:, text_rows:, :local_heads]
    key_acc = projected[:, :, local_heads : 2 * local_heads]
    value_acc = jnp.concatenate(
        [
            projected[:, :, 2 * local_heads :],
            value_rest.reshape(micro_count, seq_rows, narrow),
        ],
        axis=2,
    )
    gain_pair = qk_gain[0]
    contract_last = (((1,), (1,)), ((), ()))
    other_out = lax.dynamic_slice_in_dim(out_cols, (1 - tp_index) * half_width, half_width, 0)
    own_out = lax.dynamic_slice_in_dim(out_cols, tp_index * half_width, half_width, 0)
    hid_half = lax.dynamic_slice_in_dim(hidden, tp_index * half_width, half_width, 2)
    gate_half = lax.dynamic_slice_in_dim(modulate[:, 2:3], tp_index * half_width, half_width, 2)
    act_halves = []
    act_rows = []
    for sample in range(micro_count):
        queries = head_norm(
            query_acc[sample].reshape(img_rows, head_count, HEAD_DIM), gain_pair[0]
        )
        keys_all = head_norm(
            key_acc[sample].reshape(seq_rows, head_count, HEAD_DIM), gain_pair[1]
        )
        values_all = value_acc[sample].reshape(seq_rows, head_count, HEAD_DIM).astype(jnp.bfloat16)
        scores = jnp.einsum(
            "ihd,jhd->hij", queries, keys_all, preferred_element_type=jnp.float32
        ) / math.sqrt(HEAD_DIM)
        attend = jax.nn.softmax(scores, axis=-1).astype(jnp.bfloat16)
        mixed_heads = jnp.einsum(
            "hij,jhd->ihd", attend, values_all, preferred_element_type=jnp.float32
        )
        mixed_heads = mixed_heads.astype(jnp.bfloat16).reshape(img_rows, local_heads)
        other_part = lax.dot_general(
            mixed_heads, other_out, contract_last, preferred_element_type=jnp.float32
        ).astype(jnp.bfloat16)
        got_part = swap(other_part, "tp")
        own_part_heads = rounded(
            lax.dot_general(mixed_heads, own_out, contract_last, preferred_element_type=jnp.float32)
        )
        head_sum = own_part_heads + got_part.astype(jnp.float32)
        act_one = hid_half[sample] + gate_half[sample] * head_sum
        act_own = act_one.astype(jnp.bfloat16)
        act_got = lax.ppermute(act_own, ("side", "tp"), [(0, 1), (1, 0)])
        act_halves.append(act_one)
        act_rows.append(
            jnp.where(
                tp_index == 0,
                jnp.concatenate([act_own, act_got], axis=1),
                jnp.concatenate([act_got, act_own], axis=1),
            )
        )
    act_half = jnp.concatenate(act_halves, axis=0)
    act_narrow = jnp.concatenate(act_rows, axis=0)
    act_other = passed_along(act_narrow, "side", 1)
    control_rows = jnp.where(is_control, act_narrow, act_other)
    own_part = block_matmul(control_rows, back, 3, 2, narrow)
    own_narrow = own_part.astype(jnp.bfloat16)
    other_narrow = partner(own_narrow, "side", 0)
    residual_narrow = jnp.where(
        is_control,
        jnp.concatenate([own_narrow, other_narrow], axis=1),
        jnp.concatenate([other_narrow, own_narrow], axis=1),
    )
    merged = act_half + residual_narrow.astype(jnp.float32)
    section_out = jnp.where(is_control, residual_narrow, merged.astype(jnp.bfloat16))
    final_half = lax.dynamic_slice_in_dim(final_mod, tp_index * half_width, half_width, 2)
    merged_rows = merged.reshape(micro_count, img_rows, half_width)
    row_total, squares = lax.psum(
        (
            jnp.sum(merged_rows, axis=-1, keepdims=True),
            jnp.sum(merged_rows * merged_rows, axis=-1, keepdims=True),
        ),
        "tp",
    )
    mean_val = row_total / width_full
    spread = squares / width_full - mean_val * mean_val
    scale_inv = lax.rsqrt(spread + EPS)
    unit_rows = (merged_rows - mean_val) * scale_inv
    final_in = (unit_rows * (1.0 + final_half[:, 1:2]) + final_half[:, 0:1]).astype(jnp.bfloat16)
    pred_part = jnp.dot(
        final_in.reshape(flat_rows, half_width), proj_weight, preferred_element_type=jnp.float32
    )
    prediction = pred_part + swap(pred_part, "tp")
    loss_factor = 4.0 / math.sqrt(micro_count * ctl_count * img_rows)
    grad_pred = (loss_factor * (prediction - velocity_target.reshape(flat_rows, -1))).astype(
        jnp.bfloat16
    )
    grad_unit = lax.dot_general(
        grad_pred, proj_weight, (((1,), (1,)), ((), ())), preferred_element_type=jnp.float32
    )
    grad_unit = grad_unit.reshape(micro_count, img_rows, half_width) * (1.0 + final_half[:, 1:2])
    first_sum, second_sum = lax.psum(
        (
            jnp.sum(grad_unit, axis=-1, keepdims=True),
            jnp.sum(grad_unit * unit_rows, axis=-1, keepdims=True),
        ),
        "tp",
    )
    grad_narrow = (
        (grad_unit - first_sum / width_full - unit_rows * (second_sum / width_full)) * scale_inv
    ).astype(jnp.bfloat16)
    grad_narrow = grad_narrow.reshape(flat_rows, half_width)
    returned = passed_along(grad_narrow, "side", -1)
    grad_rows_all = jnp.where(is_control, returned, grad_narrow)
    own_act = lax.dynamic_index_in_dim(
        control_rows.reshape(flat_rows, ctl_count, 2, block_rows), side_index, 2, keepdims=False
    )
    own_act = own_act.reshape(flat_rows, ctl_count * block_rows)
    product = lax.dot_general(
        own_act, grad_rows_all, (((0,), (0,)), ((), ())), preferred_element_type=jnp.float32
    )
    group_parts = rounded(product).astype(jnp.bfloat16).reshape(ctl_count, block_rows, half_width)
    received = lax.all_to_all(group_parts, "ctl", 0, 0, tiled=True)
    zero_grad = jnp.sum(received.astype(jnp.float32), axis=0)
    return (section_out.reshape(1, micro_count, img_rows, half_width), zero_grad)


def solution(mesh):
    return jax.shard_map(
        local,
        mesh=mesh,
        in_specs=(
            P("ctl", None, None),
            P("ctl", None, None),
            P("ctl", None),
            P("ctl", None, None),
            P("ctl"),
            P("side", "ctl", None, None),
            P("side", "ctl", None, "tp"),
            P("side", None, None),
            P("side", "tp", "ctl"),
            P("ctl", "tp"),
            P("tp", None),
            P("ctl", None, None),
            P("ctl", None, None),
        ),
        out_specs=(P("side", "ctl", None, "tp"), P(("ctl", "side"), "tp")),
        check_vma=False,
    )
```

```python
import math

import jax
import jax.numpy as jnp
from jax import lax
from jax.experimental import pallas as pl
from jax.sharding import PartitionSpec as P

HEAD_DIM = 128


EPS = 1e-06


def passed_along(shard, axis, by):
    length = lax.axis_size(axis)
    pairs = [(i, i + by) for i in range(length) if 0 <= i + by < length]
    return lax.ppermute(shard, axis, pairs)


def partner(value, axis, bit):
    mask = 2**bit
    pairs = [(source, source ^ mask) for source in range(lax.axis_size(axis))]
    return lax.ppermute(value, axis, pairs)


CTL_SHAPE = (4, 2, 4)


def ctl_coords(index):
    _, count_z, count_x = CTL_SHAPE
    return index // (count_z * count_x), (index // count_x) % count_z, index % count_x


def ctl_shift(value, step_y, flip_z, step_x):
    count_y, count_z, count_x = CTL_SHAPE
    pairs = []
    for source in range(count_y * count_z * count_x):
        at_y, at_z, at_x = ctl_coords(source)
        target = ((at_y + step_y) % count_y * count_z + (at_z ^ flip_z)) * count_x + (at_x + step_x) % count_x
        pairs.append((source, target))
    return lax.ppermute(value, "ctl", pairs)


def ring_stage(block, along_y, position):
    step = (1, 0) if along_y else (0, 1)
    forward = lambda value: ctl_shift(value, step[0], 0, step[1])
    backward = lambda value: ctl_shift(value, -step[0], 0, -step[1])
    from_before = forward(block)
    from_after = backward(block)
    half = block.shape[0] // 2
    far = jnp.concatenate([backward(from_after[:half]), forward(from_before[half:])], axis=0)
    relative = jnp.stack([block, from_after, far, from_before])
    return jnp.roll(relative, position, axis=0)


def ctl_gather(piece):
    at_y, at_z, at_x = ctl_coords(lax.axis_index("ctl"))
    rows, width = piece.shape
    paired = ctl_shift(piece, 0, 1, 0)
    pair = jnp.where(at_z == 0, jnp.stack([piece, paired]), jnp.stack([paired, piece]))
    split = width // 2
    first = ring_stage(pair[..., :split], False, at_x)
    first = ring_stage(jnp.swapaxes(first, 0, 1), True, at_y)
    second = ring_stage(pair[..., split:], True, at_y)
    second = ring_stage(second, False, at_x)
    second = jnp.moveaxis(second, 0, 2)
    return first.reshape(-1, split), second.reshape(-1, width - split)


def swap(value, axis):
    return lax.ppermute(value, axis, [(0, 1), (1, 0)])


def block_matmul(rows, weight, first_block, block_count, width):
    row_count, depth = rows.shape

    def kernel(rows_ref, weight_ref, out_ref):
        out_ref[...] = jnp.dot(rows_ref[...], weight_ref[...], preferred_element_type=jnp.float32)

    return pl.pallas_call(
        kernel,
        grid=(block_count,),
        in_specs=[
            pl.BlockSpec((row_count, depth), lambda n: (0, 0)),
            pl.BlockSpec((depth, width), lambda n: (0, first_block + n)),
        ],
        out_specs=pl.BlockSpec((row_count, width), lambda n: (0, n)),
        out_shape=jax.ShapeDtypeStruct((row_count, block_count * width), jnp.float32),
        cost_estimate=pl.CostEstimate(
            flops=2 * row_count * depth * block_count * width,
            transcendentals=0,
            bytes_accessed=2 * depth * (row_count + block_count * width)
            + 4 * row_count * block_count * width,
        ),
    )(rows, weight)


def layer_norm(values):
    center = values - jnp.mean(values, axis=-1, keepdims=True)
    spread = jnp.mean(center * center, axis=-1, keepdims=True)
    return center * lax.rsqrt(spread + EPS)


def head_norm(values, gain_row):
    power_mean = jnp.mean(values * values, axis=-1, keepdims=True)
    return (values * lax.rsqrt(power_mean + EPS) * gain_row).astype(jnp.bfloat16)


def rounded(values):
    narrow = lax.optimization_barrier(values.astype(jnp.bfloat16))
    return narrow.astype(jnp.float32)


def local(
    image_latent,
    control_latent,
    control_order,
    captions,
    caption_ids,
    modulation,
    qkv_weight,
    qk_gain,
    out_weight,
    zero_weight,
    proj_weight,
    final_mod,
    velocity_target,
):
    side_index = lax.axis_index("side")
    tp_index = lax.axis_index("tp")
    ctl_count = lax.axis_size("ctl")
    tp_count = lax.axis_size("tp")
    is_control = side_index == 0
    micro_count, img_rows, width_full = image_latent.shape
    text_rows = captions.shape[1]
    seq_rows = text_rows + img_rows
    local_heads = qkv_weight.shape[3]
    head_count = local_heads // HEAD_DIM
    half_width = width_full // tp_count
    quarter_width = half_width // 2
    flat_rows = micro_count * img_rows
    block_rows = width_full // (2 * ctl_count)
    token_ids = lax.broadcasted_iota(jnp.int32, (micro_count, img_rows, img_rows), 2)
    picks = (control_order[:, :, None] == token_ids).astype(jnp.bfloat16)
    aligned = jnp.einsum(
        "bij,bjd->bid", picks, control_latent, preferred_element_type=jnp.float32
    ).astype(jnp.bfloat16)
    plain_rows = image_latent.astype(jnp.float32)
    hidden = plain_rows + jnp.where(is_control, 1.0, 0.0) * aligned.astype(jnp.float32)
    chosen = jnp.take(captions, caption_ids, axis=0).astype(jnp.float32)
    sequence = jnp.concatenate([chosen, hidden], axis=1)
    modulate = modulation[0]
    normed = (layer_norm(sequence) * (1.0 + modulate[:, 1:2]) + modulate[:, 0:1]).astype(
        jnp.bfloat16
    )
    text_flat = normed.reshape(micro_count * seq_rows, width_full)
    image_flat = normed[:, text_rows:].reshape(flat_rows, width_full)
    local_rows = qkv_weight.shape[1]
    own_cols = lax.dynamic_slice_in_dim(zero_weight, side_index * quarter_width, quarter_width, 1)
    packed = jnp.concatenate(
        [
            qkv_weight[0].reshape(local_rows, 3 * local_heads),
            out_weight[0].T,
            own_cols,
        ],
        axis=1,
    )
    front, back = ctl_gather(packed)
    count_rows = front.shape[0]
    narrow = local_heads // 2
    front_blocks = front.shape[1] // narrow
    out_cols = back[:, narrow : narrow + local_heads]
    projected = block_matmul(text_flat, front, 0, front_blocks, narrow)
    value_rest = block_matmul(text_flat, back, 0, 1, narrow)
    projected = projected.reshape(micro_count, seq_rows, front_blocks * narrow)
    query_acc = projected[:, text_rows:, :local_heads]
    key_acc = projected[:, :, local_heads : 2 * local_heads]
    value_acc = jnp.concatenate(
        [
            projected[:, :, 2 * local_heads :],
            value_rest.reshape(micro_count, seq_rows, narrow),
        ],
        axis=2,
    )
    gain_pair = qk_gain[0]
    contract_last = (((1,), (1,)), ((), ()))
    other_out = lax.dynamic_slice_in_dim(out_cols, (1 - tp_index) * half_width, half_width, 0)
    own_out = lax.dynamic_slice_in_dim(out_cols, tp_index * half_width, half_width, 0)
    hid_half = lax.dynamic_slice_in_dim(hidden, tp_index * half_width, half_width, 2)
    gate_half = lax.dynamic_slice_in_dim(modulate[:, 2:3], tp_index * half_width, half_width, 2)
    act_halves = []
    act_rows = []
    for sample in range(micro_count):
        queries = head_norm(
            query_acc[sample].reshape(img_rows, head_count, HEAD_DIM), gain_pair[0]
        )
        keys_all = head_norm(
            key_acc[sample].reshape(seq_rows, head_count, HEAD_DIM), gain_pair[1]
        )
        values_all = value_acc[sample].reshape(seq_rows, head_count, HEAD_DIM).astype(jnp.bfloat16)
        scores = jnp.einsum(
            "ihd,jhd->hij", queries, keys_all, preferred_element_type=jnp.float32
        ) / math.sqrt(HEAD_DIM)
        attend = jax.nn.softmax(scores, axis=-1).astype(jnp.bfloat16)
        mixed_heads = jnp.einsum(
            "hij,jhd->ihd", attend, values_all, preferred_element_type=jnp.float32
        )
        mixed_heads = mixed_heads.astype(jnp.bfloat16).reshape(img_rows, local_heads)
        other_part = lax.dot_general(
            mixed_heads, other_out, contract_last, preferred_element_type=jnp.float32
        ).astype(jnp.bfloat16)
        got_part = swap(other_part, "tp")
        own_part_heads = rounded(
            lax.dot_general(mixed_heads, own_out, contract_last, preferred_element_type=jnp.float32)
        )
        head_sum = own_part_heads + got_part.astype(jnp.float32)
        act_one = hid_half[sample] + gate_half[sample] * head_sum
        act_own = act_one.astype(jnp.bfloat16)
        act_got = lax.ppermute(act_own, ("side", "tp"), [(0, 1), (1, 0)])
        act_halves.append(act_one)
        act_rows.append(
            jnp.where(
                tp_index == 0,
                jnp.concatenate([act_own, act_got], axis=1),
                jnp.concatenate([act_got, act_own], axis=1),
            )
        )
    act_half = jnp.concatenate(act_halves, axis=0)
    act_narrow = jnp.concatenate(act_rows, axis=0)
    act_other = passed_along(act_narrow, "side", 1)
    control_rows = jnp.where(is_control, act_narrow, act_other)
    own_part = block_matmul(control_rows, back, 3, 2, narrow)
    own_narrow = own_part.astype(jnp.bfloat16)
    other_narrow = partner(own_narrow, "side", 0)
    residual_narrow = jnp.where(
        is_control,
        jnp.concatenate([own_narrow, other_narrow], axis=1),
        jnp.concatenate([other_narrow, own_narrow], axis=1),
    )
    merged = act_half + residual_narrow.astype(jnp.float32)
    section_out = jnp.where(is_control, residual_narrow, merged.astype(jnp.bfloat16))
    final_half = lax.dynamic_slice_in_dim(final_mod, tp_index * half_width, half_width, 2)
    merged_rows = merged.reshape(micro_count, img_rows, half_width)
    row_total, squares = lax.psum(
        (
            jnp.sum(merged_rows, axis=-1, keepdims=True),
            jnp.sum(merged_rows * merged_rows, axis=-1, keepdims=True),
        ),
        "tp",
    )
    mean_val = row_total / width_full
    spread = squares / width_full - mean_val * mean_val
    scale_inv = lax.rsqrt(spread + EPS)
    unit_rows = (merged_rows - mean_val) * scale_inv
    final_in = (unit_rows * (1.0 + final_half[:, 1:2]) + final_half[:, 0:1]).astype(jnp.bfloat16)
    pred_part = jnp.dot(
        final_in.reshape(flat_rows, half_width), proj_weight, preferred_element_type=jnp.float32
    )
    prediction = pred_part + swap(pred_part, "tp")
    loss_factor = 4.0 / math.sqrt(micro_count * ctl_count * img_rows)
    grad_pred = (loss_factor * (prediction - velocity_target.reshape(flat_rows, -1))).astype(
        jnp.bfloat16
    )
    grad_unit = lax.dot_general(
        grad_pred, proj_weight, (((1,), (1,)), ((), ())), preferred_element_type=jnp.float32
    )
    grad_unit = grad_unit.reshape(micro_count, img_rows, half_width) * (1.0 + final_half[:, 1:2])
    first_sum, second_sum = lax.psum(
        (
            jnp.sum(grad_unit, axis=-1, keepdims=True),
            jnp.sum(grad_unit * unit_rows, axis=-1, keepdims=True),
        ),
        "tp",
    )
    grad_narrow = (
        (grad_unit - first_sum / width_full - unit_rows * (second_sum / width_full)) * scale_inv
    ).astype(jnp.bfloat16)
    grad_narrow = grad_narrow.reshape(flat_rows, half_width)
    returned = passed_along(grad_narrow, "side", -1)
    grad_rows_all = jnp.where(is_control, returned, grad_narrow)
    own_act = lax.dynamic_index_in_dim(
        control_rows.reshape(flat_rows, ctl_count, 2, block_rows), side_index, 2, keepdims=False
    )
    own_act = own_act.reshape(flat_rows, ctl_count * block_rows)
    product = lax.dot_general(
        own_act, grad_rows_all, (((0,), (0,)), ((), ())), preferred_element_type=jnp.float32
    )
    group_parts = rounded(product).astype(jnp.bfloat16).reshape(ctl_count, block_rows, half_width)
    received = lax.all_to_all(group_parts, "ctl", 0, 0, tiled=True)
    zero_grad = jnp.sum(received.astype(jnp.float32), axis=0)
    return (section_out.reshape(1, micro_count, img_rows, half_width), zero_grad)


def solution(mesh):
    return jax.shard_map(
        local,
        mesh=mesh,
        in_specs=(
            P("ctl", None, None),
            P("ctl", None, None),
            P("ctl", None),
            P("ctl", None, None),
            P("ctl"),
            P("side", "ctl", None, None),
            P("side", "ctl", None, "tp"),
            P("side", None, None),
            P("side", "tp", "ctl"),
            P("ctl", "tp"),
            P("tp", None),
            P("ctl", None, None),
            P("ctl", None, None),
        ),
        out_specs=(P("side", "ctl", None, "tp"), P(("ctl", "side"), "tp")),
        check_vma=False,
    )
```

```python
import math

import jax
import jax.numpy as jnp
from jax import lax
from jax.experimental import pallas as pl
from jax.sharding import PartitionSpec as P

HEAD_DIM = 128


EPS = 1e-06


def passed_along(shard, axis, by):
    length = lax.axis_size(axis)
    pairs = [(i, i + by) for i in range(length) if 0 <= i + by < length]
    return lax.ppermute(shard, axis, pairs)


def partner(value, axis, bit):
    mask = 2**bit
    pairs = [(source, source ^ mask) for source in range(lax.axis_size(axis))]
    return lax.ppermute(value, axis, pairs)


CTL_SHAPE = (4, 2, 4)


def ctl_coords(index):
    _, count_z, count_x = CTL_SHAPE
    return index // (count_z * count_x), (index // count_x) % count_z, index % count_x


def ctl_shift(value, step_y, flip_z, step_x):
    count_y, count_z, count_x = CTL_SHAPE
    pairs = []
    for source in range(count_y * count_z * count_x):
        at_y, at_z, at_x = ctl_coords(source)
        target = ((at_y + step_y) % count_y * count_z + (at_z ^ flip_z)) * count_x + (at_x + step_x) % count_x
        pairs.append((source, target))
    return lax.ppermute(value, "ctl", pairs)


def ring_stage(block, along_y, position):
    step = (1, 0) if along_y else (0, 1)
    forward = lambda value: ctl_shift(value, step[0], 0, step[1])
    backward = lambda value: ctl_shift(value, -step[0], 0, -step[1])
    from_before = forward(block)
    from_after = backward(block)
    half = block.shape[0] // 2
    far = jnp.concatenate([backward(from_after[:half]), forward(from_before[half:])], axis=0)
    relative = jnp.stack([block, from_after, far, from_before])
    return jnp.roll(relative, position, axis=0)


def ctl_gather(piece):
    at_y, at_z, at_x = ctl_coords(lax.axis_index("ctl"))
    rows, width = piece.shape
    paired = ctl_shift(piece, 0, 1, 0)
    pair = jnp.where(at_z == 0, jnp.stack([piece, paired]), jnp.stack([paired, piece]))
    split = width // 2
    first = ring_stage(pair[..., :split], False, at_x)
    first = ring_stage(jnp.swapaxes(first, 0, 1), True, at_y)
    second = ring_stage(pair[..., split:], True, at_y)
    second = ring_stage(second, False, at_x)
    second = jnp.moveaxis(second, 0, 2)
    return first.reshape(-1, split), second.reshape(-1, width - split)


def swap(value, axis):
    return lax.ppermute(value, axis, [(0, 1), (1, 0)])


def block_matmul(rows, weight, first_block, block_count, width):
    row_count, depth = rows.shape

    def kernel(rows_ref, weight_ref, out_ref):
        out_ref[...] = jnp.dot(rows_ref[...], weight_ref[...], preferred_element_type=jnp.float32)

    return pl.pallas_call(
        kernel,
        grid=(block_count,),
        in_specs=[
            pl.BlockSpec((row_count, depth), lambda n: (0, 0)),
            pl.BlockSpec((depth, width), lambda n: (0, first_block + n)),
        ],
        out_specs=pl.BlockSpec((row_count, width), lambda n: (0, n)),
        out_shape=jax.ShapeDtypeStruct((row_count, block_count * width), jnp.float32),
        cost_estimate=pl.CostEstimate(
            flops=2 * row_count * depth * block_count * width,
            transcendentals=0,
            bytes_accessed=2 * depth * (row_count + block_count * width)
            + 4 * row_count * block_count * width,
        ),
    )(rows, weight)


def layer_norm(values):
    center = values - jnp.mean(values, axis=-1, keepdims=True)
    spread = jnp.mean(center * center, axis=-1, keepdims=True)
    return center * lax.rsqrt(spread + EPS)


def head_norm(values, gain_row):
    power_mean = jnp.mean(values * values, axis=-1, keepdims=True)
    return (values * lax.rsqrt(power_mean + EPS) * gain_row).astype(jnp.bfloat16)


def rounded(values):
    narrow = lax.optimization_barrier(values.astype(jnp.bfloat16))
    return narrow.astype(jnp.float32)


def local(
    image_latent,
    control_latent,
    control_order,
    captions,
    caption_ids,
    modulation,
    qkv_weight,
    qk_gain,
    out_weight,
    zero_weight,
    proj_weight,
    final_mod,
    velocity_target,
):
    side_index = lax.axis_index("side")
    tp_index = lax.axis_index("tp")
    ctl_count = lax.axis_size("ctl")
    tp_count = lax.axis_size("tp")
    is_control = side_index == 0
    micro_count, img_rows, width_full = image_latent.shape
    text_rows = captions.shape[1]
    seq_rows = text_rows + img_rows
    local_heads = qkv_weight.shape[3]
    head_count = local_heads // HEAD_DIM
    half_width = width_full // tp_count
    quarter_width = half_width // 2
    flat_rows = micro_count * img_rows
    block_rows = width_full // (2 * ctl_count)
    token_ids = lax.broadcasted_iota(jnp.int32, (micro_count, img_rows, img_rows), 2)
    picks = (control_order[:, :, None] == token_ids).astype(jnp.bfloat16)
    aligned = jnp.einsum(
        "bij,bjd->bid", picks, control_latent, preferred_element_type=jnp.float32
    ).astype(jnp.bfloat16)
    plain_rows = image_latent.astype(jnp.float32)
    hidden = plain_rows + jnp.where(is_control, 1.0, 0.0) * aligned.astype(jnp.float32)
    caption_slots = lax.broadcasted_iota(jnp.int32, (micro_count, captions.shape[0]), 1)
    caption_picks = (caption_ids[:, None] == caption_slots).astype(jnp.bfloat16)
    chosen = jnp.einsum(
        "bc,ctd->btd", caption_picks, captions, preferred_element_type=jnp.float32
    )
    sequence = jnp.concatenate([chosen, hidden], axis=1)
    modulate = modulation[0]
    normed = (layer_norm(sequence) * (1.0 + modulate[:, 1:2]) + modulate[:, 0:1]).astype(
        jnp.bfloat16
    )
    text_flat = normed.reshape(micro_count * seq_rows, width_full)
    image_flat = normed[:, text_rows:].reshape(flat_rows, width_full)
    local_rows = qkv_weight.shape[1]
    own_cols = lax.dynamic_slice_in_dim(zero_weight, side_index * quarter_width, quarter_width, 1)
    packed = jnp.concatenate(
        [
            qkv_weight[0].reshape(local_rows, 3 * local_heads),
            out_weight[0].T,
            own_cols,
        ],
        axis=1,
    )
    front, back = ctl_gather(packed)
    count_rows = front.shape[0]
    narrow = local_heads // 2
    front_blocks = front.shape[1] // narrow
    out_cols = back[:, narrow : narrow + local_heads]
    projected = block_matmul(text_flat, front, 0, front_blocks, narrow)
    value_rest = block_matmul(text_flat, back, 0, 1, narrow)
    projected = projected.reshape(micro_count, seq_rows, front_blocks * narrow)
    query_acc = projected[:, text_rows:, :local_heads]
    key_acc = projected[:, :, local_heads : 2 * local_heads]
    value_acc = jnp.concatenate(
        [
            projected[:, :, 2 * local_heads :],
            value_rest.reshape(micro_count, seq_rows, narrow),
        ],
        axis=2,
    )
    gain_pair = qk_gain[0]
    contract_last = (((1,), (1,)), ((), ()))
    other_out = lax.dynamic_slice_in_dim(out_cols, (1 - tp_index) * half_width, half_width, 0)
    own_out = lax.dynamic_slice_in_dim(out_cols, tp_index * half_width, half_width, 0)
    hid_half = lax.dynamic_slice_in_dim(hidden, tp_index * half_width, half_width, 2)
    gate_half = lax.dynamic_slice_in_dim(modulate[:, 2:3], tp_index * half_width, half_width, 2)
    act_halves = []
    act_rows = []
    for sample in range(micro_count):
        queries = head_norm(
            query_acc[sample].reshape(img_rows, head_count, HEAD_DIM), gain_pair[0]
        )
        keys_all = head_norm(
            key_acc[sample].reshape(seq_rows, head_count, HEAD_DIM), gain_pair[1]
        )
        values_all = value_acc[sample].reshape(seq_rows, head_count, HEAD_DIM).astype(jnp.bfloat16)
        scores = jnp.einsum(
            "ihd,jhd->hij", queries, keys_all, preferred_element_type=jnp.float32
        ) / math.sqrt(HEAD_DIM)
        attend = jax.nn.softmax(scores, axis=-1).astype(jnp.bfloat16)
        mixed_heads = jnp.einsum(
            "hij,jhd->ihd", attend, values_all, preferred_element_type=jnp.float32
        )
        mixed_heads = mixed_heads.astype(jnp.bfloat16).reshape(img_rows, local_heads)
        other_part = lax.dot_general(
            mixed_heads, other_out, contract_last, preferred_element_type=jnp.float32
        ).astype(jnp.bfloat16)
        got_part = swap(other_part, "tp")
        own_part_heads = rounded(
            lax.dot_general(mixed_heads, own_out, contract_last, preferred_element_type=jnp.float32)
        )
        head_sum = own_part_heads + got_part.astype(jnp.float32)
        act_one = hid_half[sample] + gate_half[sample] * head_sum
        act_own = act_one.astype(jnp.bfloat16)
        act_got = lax.ppermute(act_own, ("side", "tp"), [(0, 1), (1, 0)])
        act_halves.append(act_one)
        act_rows.append(
            jnp.where(
                tp_index == 0,
                jnp.concatenate([act_own, act_got], axis=1),
                jnp.concatenate([act_got, act_own], axis=1),
            )
        )
    act_half = jnp.concatenate(act_halves, axis=0)
    act_narrow = jnp.concatenate(act_rows, axis=0)
    act_other = passed_along(act_narrow, "side", 1)
    control_rows = jnp.where(is_control, act_narrow, act_other)
    own_part = block_matmul(control_rows, back, 3, 2, narrow)
    own_narrow = own_part.astype(jnp.bfloat16)
    other_narrow = partner(own_narrow, "side", 0)
    residual_narrow = jnp.where(
        is_control,
        jnp.concatenate([own_narrow, other_narrow], axis=1),
        jnp.concatenate([other_narrow, own_narrow], axis=1),
    )
    merged = act_half + residual_narrow.astype(jnp.float32)
    section_out = jnp.where(is_control, residual_narrow, merged.astype(jnp.bfloat16))
    final_half = lax.dynamic_slice_in_dim(final_mod, tp_index * half_width, half_width, 2)
    merged_rows = merged.reshape(micro_count, img_rows, half_width)
    row_total, squares = lax.psum(
        (
            jnp.sum(merged_rows, axis=-1, keepdims=True),
            jnp.sum(merged_rows * merged_rows, axis=-1, keepdims=True),
        ),
        "tp",
    )
    mean_val = row_total / width_full
    spread = squares / width_full - mean_val * mean_val
    scale_inv = lax.rsqrt(spread + EPS)
    unit_rows = (merged_rows - mean_val) * scale_inv
    final_in = (unit_rows * (1.0 + final_half[:, 1:2]) + final_half[:, 0:1]).astype(jnp.bfloat16)
    pred_part = jnp.dot(
        final_in.reshape(flat_rows, half_width), proj_weight, preferred_element_type=jnp.float32
    )
    prediction = pred_part + swap(pred_part, "tp")
    loss_factor = 4.0 / math.sqrt(micro_count * ctl_count * img_rows)
    grad_pred = (loss_factor * (prediction - velocity_target.reshape(flat_rows, -1))).astype(
        jnp.bfloat16
    )
    grad_unit = lax.dot_general(
        grad_pred, proj_weight, (((1,), (1,)), ((), ())), preferred_element_type=jnp.float32
    )
    grad_unit = grad_unit.reshape(micro_count, img_rows, half_width) * (1.0 + final_half[:, 1:2])
    first_sum, second_sum = lax.psum(
        (
            jnp.sum(grad_unit, axis=-1, keepdims=True),
            jnp.sum(grad_unit * unit_rows, axis=-1, keepdims=True),
        ),
        "tp",
    )
    grad_narrow = (
        (grad_unit - first_sum / width_full - unit_rows * (second_sum / width_full)) * scale_inv
    ).astype(jnp.bfloat16)
    grad_narrow = grad_narrow.reshape(flat_rows, half_width)
    returned = passed_along(grad_narrow, "side", -1)
    grad_rows_all = jnp.where(is_control, returned, grad_narrow)
    own_act = lax.dynamic_index_in_dim(
        control_rows.reshape(flat_rows, ctl_count, 2, block_rows), side_index, 2, keepdims=False
    )
    own_act = own_act.reshape(flat_rows, ctl_count * block_rows)
    product = lax.dot_general(
        own_act, grad_rows_all, (((0,), (0,)), ((), ())), preferred_element_type=jnp.float32
    )
    group_parts = rounded(product).astype(jnp.bfloat16).reshape(ctl_count, block_rows, half_width)
    received = lax.all_to_all(group_parts, "ctl", 0, 0, tiled=True)
    zero_grad = jnp.sum(received.astype(jnp.float32), axis=0)
    return (section_out.reshape(1, micro_count, img_rows, half_width), zero_grad)


def solution(mesh):
    return jax.shard_map(
        local,
        mesh=mesh,
        in_specs=(
            P("ctl", None, None),
            P("ctl", None, None),
            P("ctl", None),
            P("ctl", None, None),
            P("ctl"),
            P("side", "ctl", None, None),
            P("side", "ctl", None, "tp"),
            P("side", None, None),
            P("side", "tp", "ctl"),
            P("ctl", "tp"),
            P("tp", None),
            P("ctl", None, None),
            P("ctl", None, None),
        ),
        out_specs=(P("side", "ctl", None, "tp"), P(("ctl", "side"), "tp")),
        check_vma=False,
    )
```

```python
import math

import jax
import jax.numpy as jnp
from jax import lax
from jax.experimental import pallas as pl
from jax.sharding import PartitionSpec as P

HEAD_DIM = 128


EPS = 1e-06


def passed_along(shard, axis, by):
    length = lax.axis_size(axis)
    pairs = [(i, i + by) for i in range(length) if 0 <= i + by < length]
    return lax.ppermute(shard, axis, pairs)


def partner(value, axis, bit):
    mask = 2**bit
    pairs = [(source, source ^ mask) for source in range(lax.axis_size(axis))]
    return lax.ppermute(value, axis, pairs)


CTL_SHAPE = (4, 2, 4)


def ctl_coords(index):
    _, count_z, count_x = CTL_SHAPE
    return index // (count_z * count_x), (index // count_x) % count_z, index % count_x


def ctl_shift(value, step_y, flip_z, step_x):
    count_y, count_z, count_x = CTL_SHAPE
    pairs = []
    for source in range(count_y * count_z * count_x):
        at_y, at_z, at_x = ctl_coords(source)
        target = ((at_y + step_y) % count_y * count_z + (at_z ^ flip_z)) * count_x + (at_x + step_x) % count_x
        pairs.append((source, target))
    return lax.ppermute(value, "ctl", pairs)


def ring_stage(block, along_y, position):
    step = (1, 0) if along_y else (0, 1)
    forward = lambda value: ctl_shift(value, step[0], 0, step[1])
    backward = lambda value: ctl_shift(value, -step[0], 0, -step[1])
    from_before = forward(block)
    from_after = backward(block)
    half = block.shape[0] // 2
    far = jnp.concatenate([backward(from_after[:half]), forward(from_before[half:])], axis=0)
    relative = jnp.stack([block, from_after, far, from_before])
    return jnp.roll(relative, position, axis=0)


def ctl_gather(piece):
    at_y, at_z, at_x = ctl_coords(lax.axis_index("ctl"))
    rows, width = piece.shape
    paired = ctl_shift(piece, 0, 1, 0)
    pair = jnp.where(at_z == 0, jnp.stack([piece, paired]), jnp.stack([paired, piece]))
    split = width // 2
    first = ring_stage(pair[..., :split], False, at_x)
    first = ring_stage(jnp.swapaxes(first, 0, 1), True, at_y)
    second = ring_stage(pair[..., split:], True, at_y)
    second = ring_stage(second, False, at_x)
    second = jnp.moveaxis(second, 0, 2)
    return first.reshape(-1, split), second.reshape(-1, width - split)


def swap(value, axis):
    return lax.ppermute(value, axis, [(0, 1), (1, 0)])


def block_matmul(rows, weight, first_block, block_count, width):
    row_count, depth = rows.shape

    def kernel(rows_ref, weight_ref, out_ref):
        out_ref[...] = jnp.dot(rows_ref[...], weight_ref[...], preferred_element_type=jnp.float32)

    return pl.pallas_call(
        kernel,
        grid=(block_count,),
        in_specs=[
            pl.BlockSpec((row_count, depth), lambda n: (0, 0)),
            pl.BlockSpec((depth, width), lambda n: (0, first_block + n)),
        ],
        out_specs=pl.BlockSpec((row_count, width), lambda n: (0, n)),
        out_shape=jax.ShapeDtypeStruct((row_count, block_count * width), jnp.float32),
        cost_estimate=pl.CostEstimate(
            flops=2 * row_count * depth * block_count * width,
            transcendentals=0,
            bytes_accessed=2 * depth * (row_count + block_count * width)
            + 4 * row_count * block_count * width,
        ),
    )(rows, weight)


def layer_norm(values):
    center = values - jnp.mean(values, axis=-1, keepdims=True)
    spread = jnp.mean(center * center, axis=-1, keepdims=True)
    return center * lax.rsqrt(spread + EPS)


def head_norm(values, gain_row):
    power_mean = jnp.mean(values * values, axis=-1, keepdims=True)
    return (values * lax.rsqrt(power_mean + EPS) * gain_row).astype(jnp.bfloat16)


def rounded(values):
    narrow = lax.optimization_barrier(values.astype(jnp.bfloat16))
    return narrow.astype(jnp.float32)


def local(
    image_latent,
    control_latent,
    control_order,
    captions,
    caption_ids,
    modulation,
    qkv_weight,
    qk_gain,
    out_weight,
    zero_weight,
    proj_weight,
    final_mod,
    velocity_target,
):
    side_index = lax.axis_index("side")
    tp_index = lax.axis_index("tp")
    ctl_count = lax.axis_size("ctl")
    tp_count = lax.axis_size("tp")
    is_control = side_index == 0
    micro_count, img_rows, width_full = image_latent.shape
    text_rows = captions.shape[1]
    seq_rows = text_rows + img_rows
    local_heads = qkv_weight.shape[3]
    head_count = local_heads // HEAD_DIM
    half_width = width_full // tp_count
    quarter_width = half_width // 2
    flat_rows = micro_count * img_rows
    block_rows = width_full // (2 * ctl_count)
    token_ids = lax.broadcasted_iota(jnp.int32, (micro_count, img_rows, img_rows), 2)
    picks = (control_order[:, :, None] == token_ids).astype(jnp.bfloat16)
    aligned = jnp.einsum(
        "bij,bjd->bid", picks, control_latent, preferred_element_type=jnp.float32
    ).astype(jnp.bfloat16)
    plain_rows = image_latent.astype(jnp.float32)
    hidden = plain_rows + jnp.where(is_control, 1.0, 0.0) * aligned.astype(jnp.float32)
    chosen = jnp.take(captions, caption_ids, axis=0).astype(jnp.float32)
    sequence = jnp.concatenate([chosen, hidden], axis=1)
    modulate = modulation[0]
    normed = (layer_norm(sequence) * (1.0 + modulate[:, 1:2]) + modulate[:, 0:1]).astype(
        jnp.bfloat16
    )
    text_flat = normed.reshape(micro_count * seq_rows, width_full)
    image_flat = normed[:, text_rows:].reshape(flat_rows, width_full)
    local_rows = qkv_weight.shape[1]
    own_cols = lax.dynamic_slice_in_dim(zero_weight, side_index * quarter_width, quarter_width, 1)
    packed = jnp.concatenate(
        [
            qkv_weight[0].reshape(local_rows, 3 * local_heads),
            out_weight[0].T,
            own_cols,
        ],
        axis=1,
    )
    front, back = ctl_gather(packed)
    count_rows = front.shape[0]
    narrow = local_heads // 2
    front_blocks = front.shape[1] // narrow
    out_cols = back[:, narrow : narrow + local_heads]
    projected = block_matmul(text_flat, front, 0, front_blocks, narrow)
    value_rest = block_matmul(text_flat, back, 0, 1, narrow)
    projected = projected.reshape(micro_count, seq_rows, front_blocks * narrow)
    query_acc = projected[:, text_rows:, :local_heads]
    key_acc = projected[:, :, local_heads : 2 * local_heads]
    value_acc = jnp.concatenate(
        [
            projected[:, :, 2 * local_heads :],
            value_rest.reshape(micro_count, seq_rows, narrow),
        ],
        axis=2,
    )
    gain_pair = qk_gain[0]
    contract_last = (((1,), (1,)), ((), ()))
    other_out = lax.dynamic_slice_in_dim(out_cols, (1 - tp_index) * half_width, half_width, 0)
    own_out = lax.dynamic_slice_in_dim(out_cols, tp_index * half_width, half_width, 0)
    hid_half = lax.dynamic_slice_in_dim(hidden, tp_index * half_width, half_width, 2)
    gate_half = lax.dynamic_slice_in_dim(modulate[:, 2:3], tp_index * half_width, half_width, 2)
    act_halves = []
    act_rows = []
    for sample in range(micro_count):
        queries = head_norm(
            query_acc[sample].reshape(img_rows, head_count, HEAD_DIM), gain_pair[0]
        )
        keys_all = head_norm(
            key_acc[sample].reshape(seq_rows, head_count, HEAD_DIM), gain_pair[1]
        )
        values_all = value_acc[sample].reshape(seq_rows, head_count, HEAD_DIM).astype(jnp.bfloat16)
        scores = jnp.einsum(
            "ihd,jhd->hij", queries, keys_all, preferred_element_type=jnp.float32
        ) / math.sqrt(HEAD_DIM)
        attend = jax.nn.softmax(scores, axis=-1).astype(jnp.bfloat16)
        mixed_heads = jnp.einsum(
            "hij,jhd->ihd", attend, values_all, preferred_element_type=jnp.float32
        )
        mixed_heads = mixed_heads.astype(jnp.bfloat16).reshape(img_rows, local_heads)
        other_part = lax.dot_general(
            mixed_heads, other_out, contract_last, preferred_element_type=jnp.float32
        ).astype(jnp.bfloat16)
        got_part = swap(other_part, "tp")
        own_part_heads = rounded(
            lax.dot_general(mixed_heads, own_out, contract_last, preferred_element_type=jnp.float32)
        )
        head_sum = own_part_heads + got_part.astype(jnp.float32)
        act_one = hid_half[sample] + gate_half[sample] * head_sum
        act_own = act_one.astype(jnp.bfloat16)
        act_got = lax.ppermute(act_own, ("side", "tp"), [(0, 1), (1, 0)])
        act_halves.append(act_one)
        act_rows.append(
            jnp.where(
                tp_index == 0,
                jnp.concatenate([act_own, act_got], axis=1),
                jnp.concatenate([act_got, act_own], axis=1),
            )
        )
    act_half = jnp.concatenate(act_halves, axis=0)
    act_narrow = jnp.concatenate(act_rows, axis=0)
    act_other = passed_along(act_narrow, "side", 1)
    control_rows = jnp.where(is_control, act_narrow, act_other)
    own_part = block_matmul(control_rows, back, 3, 2, narrow)
    own_narrow = own_part.astype(jnp.bfloat16)
    other_narrow = partner(own_narrow, "side", 0)
    residual_narrow = jnp.where(
        is_control,
        jnp.concatenate([own_narrow, other_narrow], axis=1),
        jnp.concatenate([other_narrow, own_narrow], axis=1),
    )
    merged = act_half + residual_narrow.astype(jnp.float32)
    section_out = jnp.where(is_control, residual_narrow, merged.astype(jnp.bfloat16))
    final_half = lax.dynamic_slice_in_dim(final_mod, tp_index * half_width, half_width, 2)
    merged_rows = merged.reshape(micro_count, img_rows, half_width)
    row_total, squares = lax.psum(
        (
            jnp.sum(merged_rows, axis=-1, keepdims=True),
            jnp.sum(merged_rows * merged_rows, axis=-1, keepdims=True),
        ),
        "tp",
    )
    mean_val = row_total / width_full
    spread = squares / width_full - mean_val * mean_val
    scale_inv = lax.rsqrt(spread + EPS)
    unit_rows = (merged_rows - mean_val) * scale_inv
    final_in = (unit_rows * (1.0 + final_half[:, 1:2]) + final_half[:, 0:1]).astype(jnp.bfloat16)
    pred_part = jnp.dot(
        final_in.reshape(flat_rows, half_width), proj_weight, preferred_element_type=jnp.float32
    )
    prediction = pred_part + swap(pred_part, "tp")
    loss_factor = 4.0 / math.sqrt(micro_count * ctl_count * img_rows)
    grad_pred = (loss_factor * (prediction - velocity_target.reshape(flat_rows, -1))).astype(
        jnp.bfloat16
    )
    grad_unit = lax.dot_general(
        grad_pred, proj_weight, (((1,), (1,)), ((), ())), preferred_element_type=jnp.float32
    )
    grad_unit = grad_unit.reshape(micro_count, img_rows, half_width) * (1.0 + final_half[:, 1:2])
    first_sum, second_sum = lax.psum(
        (
            jnp.sum(grad_unit, axis=-1, keepdims=True),
            jnp.sum(grad_unit * unit_rows, axis=-1, keepdims=True),
        ),
        "tp",
    )
    grad_narrow = (
        (grad_unit - first_sum / width_full - unit_rows * (second_sum / width_full)) * scale_inv
    ).astype(jnp.bfloat16)
    grad_narrow = grad_narrow.reshape(flat_rows, half_width)
    returned = passed_along(grad_narrow, "side", -1)
    grad_rows_all = jnp.where(is_control, returned, grad_narrow)
    own_act = lax.dynamic_index_in_dim(
        control_rows.reshape(flat_rows, ctl_count, 2, block_rows), side_index, 2, keepdims=False
    )
    own_act = own_act.reshape(flat_rows, ctl_count * block_rows)
    column_half = half_width // 2
    sums = []
    for part in range(2):
        product = lax.dot_general(
            own_act,
            grad_rows_all[:, part * column_half : (part + 1) * column_half],
            (((0,), (0,)), ((), ())),
            preferred_element_type=jnp.float32,
        )
        group_parts = rounded(product).astype(jnp.bfloat16)
        group_parts = group_parts.reshape(ctl_count, block_rows, column_half)
        received = lax.all_to_all(group_parts, "ctl", 0, 0, tiled=True)
        sums.append(jnp.sum(received.astype(jnp.float32), axis=0))
    zero_grad = jnp.concatenate(sums, axis=1)
    return (section_out.reshape(1, micro_count, img_rows, half_width), zero_grad)


def solution(mesh):
    return jax.shard_map(
        local,
        mesh=mesh,
        in_specs=(
            P("ctl", None, None),
            P("ctl", None, None),
            P("ctl", None),
            P("ctl", None, None),
            P("ctl"),
            P("side", "ctl", None, None),
            P("side", "ctl", None, "tp"),
            P("side", None, None),
            P("side", "tp", "ctl"),
            P("ctl", "tp"),
            P("tp", None),
            P("ctl", None, None),
            P("ctl", None, None),
        ),
        out_specs=(P("side", "ctl", None, "tp"), P(("ctl", "side"), "tp")),
        check_vma=False,
    )
```

```python
import math

import jax
import jax.numpy as jnp
from jax import lax
from jax.experimental import pallas as pl
from jax.sharding import PartitionSpec as P

HEAD_DIM = 128


EPS = 1e-06


def passed_along(shard, axis, by):
    length = lax.axis_size(axis)
    pairs = [(i, i + by) for i in range(length) if 0 <= i + by < length]
    return lax.ppermute(shard, axis, pairs)


def partner(value, axis, bit):
    mask = 2**bit
    pairs = [(source, source ^ mask) for source in range(lax.axis_size(axis))]
    return lax.ppermute(value, axis, pairs)


CTL_SHAPE = (4, 2, 4)


def ctl_coords(index):
    _, count_z, count_x = CTL_SHAPE
    return index // (count_z * count_x), (index // count_x) % count_z, index % count_x


def ctl_shift(value, step_y, flip_z, step_x):
    count_y, count_z, count_x = CTL_SHAPE
    pairs = []
    for source in range(count_y * count_z * count_x):
        at_y, at_z, at_x = ctl_coords(source)
        target = ((at_y + step_y) % count_y * count_z + (at_z ^ flip_z)) * count_x + (at_x + step_x) % count_x
        pairs.append((source, target))
    return lax.ppermute(value, "ctl", pairs)


def ring_stage(block, along_y, position):
    step = (1, 0) if along_y else (0, 1)
    forward = lambda value: ctl_shift(value, step[0], 0, step[1])
    backward = lambda value: ctl_shift(value, -step[0], 0, -step[1])
    from_before = forward(block)
    from_after = backward(block)
    half = block.shape[0] // 2
    far = jnp.concatenate([backward(from_after[:half]), forward(from_before[half:])], axis=0)
    relative = jnp.stack([block, from_after, far, from_before])
    return jnp.roll(relative, position, axis=0)


def ctl_gather(piece):
    at_y, at_z, at_x = ctl_coords(lax.axis_index("ctl"))
    rows, width = piece.shape
    paired = ctl_shift(piece, 0, 1, 0)
    pair = jnp.where(at_z == 0, jnp.stack([piece, paired]), jnp.stack([paired, piece]))
    split = width // 2
    first = ring_stage(pair[..., :split], False, at_x)
    first = ring_stage(jnp.swapaxes(first, 0, 1), True, at_y)
    second = ring_stage(pair[..., split:], True, at_y)
    second = ring_stage(second, False, at_x)
    second = jnp.moveaxis(second, 0, 2)
    return first.reshape(-1, split), second.reshape(-1, width - split)


def swap(value, axis):
    return lax.ppermute(value, axis, [(0, 1), (1, 0)])


def block_matmul(rows, weight, first_block, block_count, width):
    row_count, depth = rows.shape

    def kernel(rows_ref, weight_ref, out_ref):
        out_ref[...] = jnp.dot(rows_ref[...], weight_ref[...], preferred_element_type=jnp.float32)

    return pl.pallas_call(
        kernel,
        grid=(block_count,),
        in_specs=[
            pl.BlockSpec((row_count, depth), lambda n: (0, 0)),
            pl.BlockSpec((depth, width), lambda n: (0, first_block + n)),
        ],
        out_specs=pl.BlockSpec((row_count, width), lambda n: (0, n)),
        out_shape=jax.ShapeDtypeStruct((row_count, block_count * width), jnp.float32),
        cost_estimate=pl.CostEstimate(
            flops=2 * row_count * depth * block_count * width,
            transcendentals=0,
            bytes_accessed=2 * depth * (row_count + block_count * width)
            + 4 * row_count * block_count * width,
        ),
    )(rows, weight)


def layer_norm(values):
    center = values - jnp.mean(values, axis=-1, keepdims=True)
    spread = jnp.mean(center * center, axis=-1, keepdims=True)
    return center * lax.rsqrt(spread + EPS)


def head_norm(values, gain_row):
    power_mean = jnp.mean(values * values, axis=-1, keepdims=True)
    return (values * lax.rsqrt(power_mean + EPS) * gain_row).astype(jnp.bfloat16)


def rounded(values):
    narrow = lax.optimization_barrier(values.astype(jnp.bfloat16))
    return narrow.astype(jnp.float32)


def local(
    image_latent,
    control_latent,
    control_order,
    captions,
    caption_ids,
    modulation,
    qkv_weight,
    qk_gain,
    out_weight,
    zero_weight,
    proj_weight,
    final_mod,
    velocity_target,
):
    side_index = lax.axis_index("side")
    tp_index = lax.axis_index("tp")
    ctl_count = lax.axis_size("ctl")
    tp_count = lax.axis_size("tp")
    is_control = side_index == 0
    micro_count, img_rows, width_full = image_latent.shape
    text_rows = captions.shape[1]
    seq_rows = text_rows + img_rows
    local_heads = qkv_weight.shape[3]
    head_count = local_heads // HEAD_DIM
    half_width = width_full // tp_count
    quarter_width = half_width // 2
    flat_rows = micro_count * img_rows
    block_rows = width_full // (2 * ctl_count)
    token_ids = lax.broadcasted_iota(jnp.int32, (micro_count, img_rows, img_rows), 2)
    picks = (control_order[:, :, None] == token_ids).astype(jnp.bfloat16)
    aligned = jnp.einsum(
        "bij,bjd->bid", picks, control_latent, preferred_element_type=jnp.float32
    ).astype(jnp.bfloat16)
    plain_rows = image_latent.astype(jnp.float32)
    hidden = plain_rows + jnp.where(is_control, 1.0, 0.0) * aligned.astype(jnp.float32)
    chosen = jnp.take(captions, caption_ids, axis=0).astype(jnp.float32)
    sequence = jnp.concatenate([chosen, hidden], axis=1)
    modulate = modulation[0]
    normed = (layer_norm(sequence) * (1.0 + modulate[:, 1:2]) + modulate[:, 0:1]).astype(
        jnp.bfloat16
    )
    text_flat = normed.reshape(micro_count * seq_rows, width_full)
    image_flat = normed[:, text_rows:].reshape(flat_rows, width_full)
    local_rows = qkv_weight.shape[1]
    own_cols = lax.dynamic_slice_in_dim(zero_weight, side_index * quarter_width, quarter_width, 1)
    packed = jnp.concatenate(
        [
            qkv_weight[0].reshape(local_rows, 3 * local_heads),
            out_weight[0].T,
            own_cols,
        ],
        axis=1,
    )
    front, back = ctl_gather(packed)
    count_rows = front.shape[0]
    narrow = local_heads // 2
    front_blocks = front.shape[1] // narrow
    out_cols = back[:, narrow : narrow + local_heads]
    projected = block_matmul(text_flat, front, 0, front_blocks, narrow)
    value_rest = block_matmul(text_flat, back, 0, 1, narrow)
    projected = projected.reshape(micro_count, seq_rows, front_blocks * narrow)
    query_acc = projected[:, text_rows:, :local_heads]
    key_acc = projected[:, :, local_heads : 2 * local_heads]
    value_acc = jnp.concatenate(
        [
            projected[:, :, 2 * local_heads :],
            value_rest.reshape(micro_count, seq_rows, narrow),
        ],
        axis=2,
    )
    gain_pair = qk_gain[0]
    contract_last = (((1,), (1,)), ((), ()))
    other_out = lax.dynamic_slice_in_dim(out_cols, (1 - tp_index) * half_width, half_width, 0)
    own_out = lax.dynamic_slice_in_dim(out_cols, tp_index * half_width, half_width, 0)
    hid_half = lax.dynamic_slice_in_dim(hidden, tp_index * half_width, half_width, 2)
    gate_half = lax.dynamic_slice_in_dim(modulate[:, 2:3], tp_index * half_width, half_width, 2)
    act_halves = []
    act_rows = []
    for sample in range(micro_count):
        queries = head_norm(
            query_acc[sample].reshape(img_rows, head_count, HEAD_DIM), gain_pair[0]
        )
        keys_all = head_norm(
            key_acc[sample].reshape(seq_rows, head_count, HEAD_DIM), gain_pair[1]
        )
        values_all = value_acc[sample].reshape(seq_rows, head_count, HEAD_DIM).astype(jnp.bfloat16)
        scores = jnp.einsum(
            "ihd,jhd->hij", queries, keys_all, preferred_element_type=jnp.float32
        ) / math.sqrt(HEAD_DIM)
        attend = jax.nn.softmax(scores, axis=-1).astype(jnp.bfloat16)
        mixed_heads = jnp.einsum(
            "hij,jhd->ihd", attend, values_all, preferred_element_type=jnp.float32
        )
        mixed_heads = mixed_heads.astype(jnp.bfloat16).reshape(img_rows, local_heads)
        other_part = lax.dot_general(
            mixed_heads, other_out, contract_last, preferred_element_type=jnp.float32
        ).astype(jnp.bfloat16)
        got_part = swap(other_part, "tp")
        own_part_heads = rounded(
            lax.dot_general(mixed_heads, own_out, contract_last, preferred_element_type=jnp.float32)
        )
        head_sum = own_part_heads + got_part.astype(jnp.float32)
        act_one = hid_half[sample] + gate_half[sample] * head_sum
        act_own = act_one.astype(jnp.bfloat16)
        act_got = lax.ppermute(act_own, ("side", "tp"), [(0, 1), (1, 0)])
        act_halves.append(act_one)
        act_rows.append(
            jnp.where(
                tp_index == 0,
                jnp.concatenate([act_own, act_got], axis=1),
                jnp.concatenate([act_got, act_own], axis=1),
            )
        )
    act_half = jnp.concatenate(act_halves, axis=0)
    act_narrow = jnp.concatenate(act_rows, axis=0)
    act_other = passed_along(act_narrow, "side", 1)
    control_rows = jnp.where(is_control, act_narrow, act_other)
    own_part = block_matmul(control_rows, back, 3, 2, narrow)
    own_narrow = own_part.astype(jnp.bfloat16)
    other_narrow = partner(own_narrow, "side", 0)
    residual_narrow = jnp.where(
        is_control,
        jnp.concatenate([own_narrow, other_narrow], axis=1),
        jnp.concatenate([other_narrow, own_narrow], axis=1),
    )
    merged = act_half + residual_narrow.astype(jnp.float32)
    section_out = jnp.where(is_control, residual_narrow, merged.astype(jnp.bfloat16))
    final_half = lax.dynamic_slice_in_dim(final_mod, tp_index * half_width, half_width, 2)
    merged_rows = merged.reshape(micro_count, img_rows, half_width)
    row_total, squares = lax.psum(
        (
            jnp.sum(merged_rows, axis=-1, keepdims=True),
            jnp.sum(merged_rows * merged_rows, axis=-1, keepdims=True),
        ),
        "tp",
    )
    mean_val = row_total / width_full
    spread = squares / width_full - mean_val * mean_val
    scale_inv = lax.rsqrt(spread + EPS)
    unit_rows = (merged_rows - mean_val) * scale_inv
    final_in = (unit_rows * (1.0 + final_half[:, 1:2]) + final_half[:, 0:1]).astype(jnp.bfloat16)
    pred_part = jnp.dot(
        final_in.reshape(flat_rows, half_width), proj_weight, preferred_element_type=jnp.float32
    )
    prediction = pred_part + swap(pred_part, "tp")
    loss_factor = 4.0 / math.sqrt(micro_count * ctl_count * img_rows)
    grad_pred = (loss_factor * (prediction - velocity_target.reshape(flat_rows, -1))).astype(
        jnp.bfloat16
    )
    grad_unit = lax.dot_general(
        grad_pred, proj_weight, (((1,), (1,)), ((), ())), preferred_element_type=jnp.float32
    )
    grad_unit = grad_unit.reshape(micro_count, img_rows, half_width) * (1.0 + final_half[:, 1:2])
    first_sum, second_sum = lax.psum(
        (
            jnp.sum(grad_unit, axis=-1, keepdims=True),
            jnp.sum(grad_unit * unit_rows, axis=-1, keepdims=True),
        ),
        "tp",
    )
    grad_narrow = (
        (grad_unit - first_sum / width_full - unit_rows * (second_sum / width_full)) * scale_inv
    ).astype(jnp.bfloat16)
    grad_narrow = grad_narrow.reshape(flat_rows, half_width)
    returned = passed_along(grad_narrow, "side", -1)
    grad_rows_all = jnp.where(is_control, returned, grad_narrow)
    own_act = lax.dynamic_index_in_dim(
        control_rows.reshape(flat_rows, ctl_count, 2, block_rows), side_index, 2, keepdims=False
    )
    own_act = own_act.reshape(flat_rows, ctl_count * block_rows)
    column_half = half_width // 4
    sums = []
    for part in range(4):
        product = lax.dot_general(
            own_act,
            grad_rows_all[:, part * column_half : (part + 1) * column_half],
            (((0,), (0,)), ((), ())),
            preferred_element_type=jnp.float32,
        )
        group_parts = rounded(product).astype(jnp.bfloat16)
        group_parts = group_parts.reshape(ctl_count, block_rows, column_half)
        received = lax.all_to_all(group_parts, "ctl", 0, 0, tiled=True)
        sums.append(jnp.sum(received.astype(jnp.float32), axis=0))
    zero_grad = jnp.concatenate(sums, axis=1)
    return (section_out.reshape(1, micro_count, img_rows, half_width), zero_grad)


def solution(mesh):
    return jax.shard_map(
        local,
        mesh=mesh,
        in_specs=(
            P("ctl", None, None),
            P("ctl", None, None),
            P("ctl", None),
            P("ctl", None, None),
            P("ctl"),
            P("side", "ctl", None, None),
            P("side", "ctl", None, "tp"),
            P("side", None, None),
            P("side", "tp", "ctl"),
            P("ctl", "tp"),
            P("tp", None),
            P("ctl", None, None),
            P("ctl", None, None),
        ),
        out_specs=(P("side", "ctl", None, "tp"), P(("ctl", "side"), "tp")),
        check_vma=False,
    )
```
